512 devices in a mesh: ctx: 32 (over z, core), uly: 16 (over x, y).
Axes of the slice: x: 4, y: 4, z: 16, core: 2. Of those that a mesh axis runs over, the one named last changes fastest.
Arguments:
- query_heads: bfloat16 [1, 8192, 8192], P(None, 'ctx', 'uly'), may hold values from -2.5 to 2.5
- key_heads: bfloat16 [1, 8192, 8192], P(None, 'ctx', 'uly'), may hold values from -2.5 to 2.5
- value_heads: bfloat16 [1, 8192, 8192], P(None, 'ctx', 'uly'), may hold values from -2.5 to 2.5
- grad_out: bfloat16 [1, 8192, 8192], P(None, ('ctx', 'uly')), may hold values from -2.5 to 2.5
- log_decay: float32 [1, 64, 8192], P(None, 'uly', 'ctx'), as said below
Outputs:
- attended: bfloat16 [1, 8192, 8192], P(None, ('ctx', 'uly'))
- grad_query: bfloat16 [1, 8192, 8192], P(None, ('ctx', 'uly'))
- grad_key: bfloat16 [1, 8192, 8192], P(None, ('ctx', 'uly'))
- grad_value: bfloat16 [1, 8192, 8192], P(None, ('ctx', 'uly'))
The draws below stay inside these ranges and needn't reach their ends.
Inputs may be any that keep to these rules, and one draw needn't show every extreme that they name: `log_decay`: each entry is the logarithm of the share of a head's state that the position keeps.
All inputs are finite; a program needn't handle non-finite values.
Results may differ from the reference program's by a relative error of at most 0.0063.
Values may be sent and summed in bfloat16 or wider, within the bound.
No kernel may reach another device: no remote copies, remote signals or barrier semaphores. Data moves between devices by JAX's collectives and lax.ppermute only.
A program may use at most 64 MiB of HBM per device.

```python
import jax
import jax.numpy as jnp
from jax import lax

ATTENTION_HEADS = 64
HD = 128
BLOCK = 256
BATCH_SEQUENCES = 1
SEQUENCE_LENGTH = 8192


def draw_log_decay(key, part):
    key_sequence = jax.random.split(key, 7)
    fast_share = 0.5
    is_fast = jax.random.uniform(key_sequence[0], (BATCH_SEQUENCES, ATTENTION_HEADS, 1)) < fast_share
    fast_rate = jax.random.uniform(key_sequence[1], (BATCH_SEQUENCES, ATTENTION_HEADS, 1), minval=4.0, maxval=8.0) / BLOCK
    slow_rate = jax.random.uniform(key_sequence[2], (BATCH_SEQUENCES, ATTENTION_HEADS, 1), minval=0.05, maxval=0.4) / SEQUENCE_LENGTH
    baseline_rate = jnp.where(is_fast, fast_rate, slow_rate)
    block_count = SEQUENCE_LENGTH // BLOCK
    processor_factor = jnp.exp(jax.random.uniform(key_sequence[3], (BATCH_SEQUENCES, ATTENTION_HEADS, block_count, 1), minval=-0.7, maxval=0.7))
    processor_factor = jnp.broadcast_to(processor_factor, (BATCH_SEQUENCES, ATTENTION_HEADS, block_count, BLOCK)).reshape(BATCH_SEQUENCES, ATTENTION_HEADS, SEQUENCE_LENGTH)
    random_wobble = jax.random.uniform(key_sequence[4], (BATCH_SEQUENCES, ATTENTION_HEADS, SEQUENCE_LENGTH), minval=0.5, maxval=1.5)
    surge_position = jax.random.randint(key_sequence[5], (BATCH_SEQUENCES, ATTENTION_HEADS, 3, 1), 0, SEQUENCE_LENGTH)
    surge_penalty = jax.random.uniform(key_sequence[6], (BATCH_SEQUENCES, ATTENTION_HEADS, 3, 1), minval=0.2, maxval=0.33)
    token_position = jnp.arange(SEQUENCE_LENGTH)[None, None, None, :]
    surge_events = jnp.sum(jnp.where(token_position == surge_position, -jnp.log1p(-surge_penalty), 0.0), axis=2)
    return (-(baseline_rate * processor_factor * random_wobble) - surge_events).astype(jnp.float32)


def block_scale(key, shape, cuts, least, high):
    factor_of = 1.0
    for axis_at, shards_of in cuts:
        heights = jax.random.uniform(jax.random.fold_in(jax.random.fold_in(key, 6), axis_at), (shards_of,), jnp.float32, least / len(cuts), high / len(cuts))
        factor_of = factor_of * jnp.repeat(jnp.exp(heights), shape[axis_at] // shards_of).reshape((-1,) + (1,) * (len(shape) - 1 - axis_at))
    return factor_of


def noise(stream_key, dims, scale, limit, cuts=(), kind=jnp.bfloat16):
    values = jax.random.normal(stream_key, dims, jnp.float32) * scale
    if len(cuts) > 0:
        values = block_scale(stream_key, dims, cuts, -0.22, 0.18) * values
    return jnp.clip(values, min=-limit, max=limit).astype(kind)


def setup_inputs(seed: int = 0) -> dict:
    key_list = jax.random.split(jax.random.key(seed), 6)
    query_heads = noise(key_list[0], (BATCH_SEQUENCES, SEQUENCE_LENGTH, ATTENTION_HEADS * HD), ((HD * BLOCK) ** -0.1666667), 2.5, ((1, 32), (2, 16)))
    key_heads = noise(key_list[1], (BATCH_SEQUENCES, SEQUENCE_LENGTH, ATTENTION_HEADS * HD), ((HD * BLOCK) ** -0.1666667), 2.5, ((1, 32), (2, 16)))
    value_heads = noise(key_list[2], (BATCH_SEQUENCES, SEQUENCE_LENGTH, ATTENTION_HEADS * HD), ((HD * BLOCK) ** -0.1666667), 2.5, ((1, 32), (2, 16)))
    grad_out = noise(key_list[3], (BATCH_SEQUENCES, SEQUENCE_LENGTH, ATTENTION_HEADS * HD), ((HD * BLOCK) ** -0.1666667), 2.5, ((1, 512),))
    log_decay = draw_log_decay(jax.random.fold_in(key_list[5], 71), 0)
    return dict(query_heads=query_heads, key_heads=key_heads, value_heads=value_heads, grad_out=grad_out, log_decay=log_decay)


def as_float(array):
    return array.astype(jnp.float32)


def decay_tables(log_decay):
    cumulative = jnp.cumsum(log_decay, axis=-1)
    last_cum = cumulative[..., -1:]
    block_len = log_decay.shape[-1]
    row_ids = lax.broadcasted_iota(jnp.int32, (block_len, block_len), 0)
    col_ids = lax.broadcasted_iota(jnp.int32, (block_len, block_len), 1)
    lower_tri = row_ids >= col_ids
    spread = cumulative[..., :, None] - cumulative[..., None, :]
    decay_mask = jnp.where(lower_tri, jnp.exp(jnp.where(lower_tri, spread, 0.0)), 0.0)
    return cumulative, last_cum, decay_mask


def to_rows(table):
    return jnp.swapaxes(table, 1, 2)[..., None]


def reference(query_heads, key_heads, value_heads, grad_out, log_decay):
    block_count = SEQUENCE_LENGTH // BLOCK
    width_all = ATTENTION_HEADS * HD

    def split_blocks(array):
        return jnp.transpose(array.reshape(BATCH_SEQUENCES, block_count, BLOCK, ATTENTION_HEADS, HD), (1, 0, 2, 3, 4))

    def merge_blocks(array):
        return jnp.transpose(array, (1, 0, 2, 3, 4)).reshape(BATCH_SEQUENCES, SEQUENCE_LENGTH, width_all)

    q_blocks = split_blocks(query_heads)
    k_blocks = split_blocks(key_heads)
    v_blocks = split_blocks(value_heads)
    g_blocks = split_blocks(grad_out)
    d_blocks = jnp.transpose(log_decay.reshape(BATCH_SEQUENCES, ATTENTION_HEADS, block_count, BLOCK), (2, 0, 1, 3))

    def shared(q_block, k_block, v_block, g_block, decay_block):
        cumulative, last_cum, decay_mask = decay_tables(decay_block)
        rise_rows = to_rows(jnp.exp(cumulative))
        fall_rows = to_rows(jnp.exp(last_cum - cumulative))
        scaled_query = (rise_rows * as_float(q_block)).astype(jnp.bfloat16)
        scaled_key = (fall_rows * as_float(k_block)).astype(jnp.bfloat16)
        scores = jnp.einsum('bihd,bjhd->bhij', as_float(q_block), as_float(k_block))
        attn_weights = (scores * decay_mask).astype(jnp.bfloat16)
        grad_raw = jnp.einsum('bihe,bjhe->bhij', as_float(g_block), as_float(v_block))
        grad_scores = (grad_raw * decay_mask).astype(jnp.bfloat16)
        block_keep = jnp.exp(last_cum[..., 0])
        return rise_rows, fall_rows, scaled_query, scaled_key, attn_weights, grad_scores, block_keep

    def forward_step(state, inputs):
        q_block, k_block, v_block, g_block, decay_block = inputs
        rise_rows, fall_rows, scaled_query, scaled_key, attn_weights, grad_scores, block_keep = shared(*inputs)
        state_b = state.astype(jnp.bfloat16)
        attended = jnp.einsum('bhij,bjhd->bihd', as_float(attn_weights), as_float(v_block))
        attended = attended + jnp.einsum('bihd,bhde->bihe', as_float(scaled_query), as_float(state_b))
        grad_query = jnp.einsum('bhij,bjhd->bihd', as_float(grad_scores), as_float(k_block))
        grad_query = grad_query + rise_rows * jnp.einsum('bihe,bhde->bihd', as_float(g_block), as_float(state_b))
        update = jnp.einsum('bjhd,bjhe->bhde', as_float(scaled_key), as_float(v_block))
        new_state = block_keep[..., None, None] * state + update
        return new_state, (attended.astype(jnp.bfloat16), grad_query.astype(jnp.bfloat16))

    def backward_step(carried, inputs):
        q_block, k_block, v_block, g_block, decay_block = inputs
        rise_rows, fall_rows, scaled_query, scaled_key, attn_weights, grad_scores, block_keep = shared(*inputs)
        carried_b = carried.astype(jnp.bfloat16)
        grad_key = jnp.einsum('bhij,bihd->bjhd', as_float(grad_scores), as_float(q_block))
        grad_key = grad_key + fall_rows * jnp.einsum('bjhe,bhde->bjhd', as_float(v_block), as_float(carried_b))
        grad_value = jnp.einsum('bhij,bihe->bjhe', as_float(attn_weights), as_float(g_block))
        grad_value = grad_value + fall_rows * jnp.einsum('bjhd,bhde->bjhe', as_float(k_block), as_float(carried_b))
        local_grad = jnp.einsum('bihd,bihe->bhde', as_float(scaled_query), as_float(g_block))
        new_carried = block_keep[..., None, None] * carried + local_grad
        return new_carried, (grad_key.astype(jnp.bfloat16), grad_value.astype(jnp.bfloat16))

    inputs_all = (q_blocks, k_blocks, v_blocks, g_blocks, d_blocks)
    zero_state = jnp.zeros((BATCH_SEQUENCES, ATTENTION_HEADS, HD, HD), jnp.float32)
    final_state, forward_outs = lax.scan(forward_step, zero_state, inputs_all)
    first_carried, backward_outs = lax.scan(backward_step, zero_state, inputs_all, reverse=True)
    return (merge_blocks(forward_outs[0]), merge_blocks(forward_outs[1]),
            merge_blocks(backward_outs[0]), merge_blocks(backward_outs[1]))
```

```python
import jax
import jax.numpy as jnp
from jax import lax
from jax.sharding import PartitionSpec as P


def decay_tables(log_decay):
    cumulative = jnp.cumsum(log_decay, axis=-1)
    last_cum = cumulative[..., -1:]
    block_len = log_decay.shape[-1]
    row_ids = lax.broadcasted_iota(jnp.int32, (block_len, block_len), 0)
    col_ids = lax.broadcasted_iota(jnp.int32, (block_len, block_len), 1)
    lower_tri = row_ids >= col_ids
    spread = cumulative[..., :, None] - cumulative[..., None, :]
    decay_mask = jnp.where(lower_tri, jnp.exp(jnp.where(lower_tri, spread, 0.0)), 0.0)
    return (cumulative, last_cum, decay_mask)


def to_rows(table):
    return jnp.swapaxes(table, 1, 2)[..., None]


def to_pieces(state, count):
    batch_count, head_count, width, _ = state.shape
    banded = state.reshape(batch_count, head_count, count, width // count, width)
    return jnp.transpose(banded, (2, 0, 1, 3, 4))


def from_pieces(pieces):
    count, batch_count, head_count, rows, width = pieces.shape
    return jnp.transpose(pieces, (1, 2, 0, 3, 4)).reshape(batch_count, head_count, count * rows, width)


def block_weights(last_all):
    count = last_all.shape[0]
    inclusive = jnp.cumsum(last_all, axis=0)
    exclusive = inclusive - last_all
    inc = jnp.transpose(inclusive, (1, 2, 0))
    exc = jnp.transpose(exclusive, (1, 2, 0))
    row_ids = lax.broadcasted_iota(jnp.int32, (count, count), 0)
    col_ids = lax.broadcasted_iota(jnp.int32, (count, count), 1)
    earlier = col_ids < row_ids
    later = col_ids > row_ids
    forward_gap = exc[..., :, None] - inc[..., None, :]
    backward_gap = exc[..., None, :] - inc[..., :, None]
    forward = jnp.where(earlier, jnp.exp(jnp.where(earlier, forward_gap, 0.0)), 0.0)
    backward = jnp.where(later, jnp.exp(jnp.where(later, backward_gap, 0.0)), 0.0)
    return forward, backward


def mix_blocks(weights, pieces):
    return jnp.einsum(
        "bhcd,dbhrx->cbhrx", weights, pieces, precision=lax.Precision.HIGHEST,
        preferred_element_type=jnp.float32,
    )


def local(query_heads, key_heads, value_heads, grad_out, log_decay):
    batch_count, positions, width_heads = query_heads.shape
    head_count = log_decay.shape[1]
    width = width_heads // head_count
    uly_count = lax.axis_size("uly")
    ctx_count = lax.axis_size("ctx")
    head_shape = (batch_count, positions, head_count, width)
    q_split = query_heads.reshape(head_shape)
    k_split = key_heads.reshape(head_shape)
    v_split = value_heads.reshape(head_shape)

    rows_in = grad_out.shape[1]
    g_parts = grad_out.reshape(batch_count, rows_in, uly_count, width_heads)
    g_parts = jnp.transpose(g_parts, (2, 0, 1, 3))
    g_parts = lax.all_to_all(g_parts, "uly", 0, 0, tiled=True)
    g_split = jnp.transpose(g_parts, (1, 0, 2, 3)).reshape(head_shape)

    cumulative, last_cum, decay_mask = decay_tables(log_decay)
    rise_rows = to_rows(jnp.exp(cumulative))
    fall_rows = to_rows(jnp.exp(last_cum - cumulative))
    scaled_query = (rise_rows * q_split).astype(jnp.bfloat16)
    scaled_key = (fall_rows * k_split).astype(jnp.bfloat16)
    update = jnp.einsum("bjhd,bjhe->bhde", scaled_key, v_split, preferred_element_type=jnp.float32)

    last_row = jnp.broadcast_to(last_cum, (batch_count, head_count, width))
    send = to_pieces(update, ctx_count)
    last_piece = jnp.broadcast_to(last_row[None, :, :, None, :], (ctx_count, batch_count, head_count, 1, width))
    send = jnp.concatenate([send, last_piece], axis=3)
    got = lax.all_to_all(send, "ctx", 0, 0, tiled=True)
    band = width // ctx_count
    forward_w, backward_w = block_weights(got[:, :, :, band, 0])
    state_pieces = mix_blocks(forward_w, got[:, :, :, :band, :])
    state_in = from_pieces(lax.all_to_all(state_pieces, "ctx", 0, 0, tiled=True))

    local_grad = jnp.einsum(
        "bihd,bihe->bhde", scaled_query, g_split, preferred_element_type=jnp.float32
    )
    got_grad = lax.all_to_all(to_pieces(local_grad, ctx_count), "ctx", 0, 0, tiled=True)
    carried_pieces = mix_blocks(backward_w, got_grad)
    carried = from_pieces(lax.all_to_all(carried_pieces, "ctx", 0, 0, tiled=True))

    scores = jnp.einsum("bihd,bjhd->bhij", q_split, k_split, preferred_element_type=jnp.float32)
    attn_weights = (scores * decay_mask).astype(jnp.bfloat16)
    grad_raw = jnp.einsum("bihe,bjhe->bhij", g_split, v_split, preferred_element_type=jnp.float32)
    grad_scores = (grad_raw * decay_mask).astype(jnp.bfloat16)
    state_b = state_in.astype(jnp.bfloat16)
    attended = jnp.einsum(
        "bhij,bjhd->bihd", attn_weights, v_split, preferred_element_type=jnp.float32
    )
    attended = attended + jnp.einsum(
        "bihd,bhde->bihe", scaled_query, state_b, preferred_element_type=jnp.float32
    )
    query_part = jnp.einsum(
        "bhij,bjhd->bihd", grad_scores, k_split, preferred_element_type=jnp.float32
    )
    query_part = query_part + rise_rows * jnp.einsum(
        "bihe,bhde->bihd", g_split, state_b, preferred_element_type=jnp.float32
    )
    carried_b = carried.astype(jnp.bfloat16)
    key_part = jnp.einsum(
        "bhij,bihd->bjhd", grad_scores, q_split, preferred_element_type=jnp.float32
    )
    key_part = key_part + fall_rows * jnp.einsum(
        "bjhe,bhde->bjhd", v_split, carried_b, preferred_element_type=jnp.float32
    )
    value_part = jnp.einsum(
        "bhij,bihe->bjhe", attn_weights, g_split, preferred_element_type=jnp.float32
    )
    value_part = value_part + fall_rows * jnp.einsum(
        "bjhd,bhde->bjhe", k_split, carried_b, preferred_element_type=jnp.float32
    )

    outs = jnp.stack([attended, query_part, key_part, value_part]).astype(jnp.bfloat16)
    outs = outs.reshape(4, batch_count, uly_count, positions // uly_count, width_heads)
    outs = jnp.transpose(outs, (2, 0, 1, 3, 4))
    outs = lax.all_to_all(outs, "uly", 0, 0, tiled=True)
    outs = jnp.transpose(outs, (1, 2, 3, 0, 4)).reshape(
        4, batch_count, positions // uly_count, uly_count * width_heads
    )
    return (outs[0], outs[1], outs[2], outs[3])


def solution(mesh):
    placed = (
        P(None, "ctx", "uly"),
        P(None, "ctx", "uly"),
        P(None, "ctx", "uly"),
        P(None, ("ctx", "uly"), None),
        P(None, "uly", "ctx"),
    )
    return jax.shard_map(
        local,
        mesh=mesh,
        in_specs=placed,
        out_specs=(
            P(None, ("ctx", "uly"), None),
            P(None, ("ctx", "uly"), None),
            P(None, ("ctx", "uly"), None),
            P(None, ("ctx", "uly"), None),
        ),
        check_vma=False,
    )
```

```python
import jax
import jax.numpy as jnp
from jax import lax
from jax.sharding import PartitionSpec as P


def decay_tables(log_decay):
    cumulative = jnp.cumsum(log_decay, axis=-1)
    last_cum = cumulative[..., -1:]
    block_len = log_decay.shape[-1]
    row_ids = lax.broadcasted_iota(jnp.int32, (block_len, block_len), 0)
    col_ids = lax.broadcasted_iota(jnp.int32, (block_len, block_len), 1)
    lower_tri = row_ids >= col_ids
    spread = cumulative[..., :, None] - cumulative[..., None, :]
    decay_mask = jnp.where(lower_tri, jnp.exp(jnp.where(lower_tri, spread, 0.0)), 0.0)
    return (cumulative, last_cum, decay_mask)


def to_rows(table):
    return jnp.swapaxes(table, 1, 2)[..., None]


def to_pieces(state, count):
    batch_count, head_count, width, _ = state.shape
    banded = state.reshape(batch_count, head_count, count, width // count, width)
    return jnp.transpose(banded, (2, 0, 1, 3, 4))


def from_pieces(pieces):
    count, batch_count, head_count, rows, width = pieces.shape
    return jnp.transpose(pieces, (1, 2, 0, 3, 4)).reshape(batch_count, head_count, count * rows, width)


def block_weights(last_all):
    count = last_all.shape[0]
    inclusive = jnp.cumsum(last_all, axis=0)
    exclusive = inclusive - last_all
    inc = jnp.transpose(inclusive, (1, 2, 0))
    exc = jnp.transpose(exclusive, (1, 2, 0))
    row_ids = lax.broadcasted_iota(jnp.int32, (count, count), 0)
    col_ids = lax.broadcasted_iota(jnp.int32, (count, count), 1)
    earlier = col_ids < row_ids
    later = col_ids > row_ids
    forward_gap = exc[..., :, None] - inc[..., None, :]
    backward_gap = exc[..., None, :] - inc[..., :, None]
    forward = jnp.where(earlier, jnp.exp(jnp.where(earlier, forward_gap, 0.0)), 0.0)
    backward = jnp.where(later, jnp.exp(jnp.where(later, backward_gap, 0.0)), 0.0)
    return forward, backward


def mix_blocks(weights, pieces):
    return jnp.einsum(
        "bhcd,dbhrx->cbhrx", weights, pieces, precision=lax.Precision.HIGHEST,
        preferred_element_type=jnp.float32,
    )


def local(query_heads, key_heads, value_heads, grad_out, log_decay):
    batch_count, positions, width_heads = query_heads.shape
    head_count = log_decay.shape[1]
    width = width_heads // head_count
    uly_count = lax.axis_size("uly")
    ctx_count = lax.axis_size("ctx")
    head_shape = (batch_count, positions, head_count, width)
    q_split = query_heads.reshape(head_shape)
    k_split = key_heads.reshape(head_shape)
    v_split = value_heads.reshape(head_shape)

    rows_in = grad_out.shape[1]
    g_parts = grad_out.reshape(batch_count, rows_in, uly_count, width_heads)
    g_parts = jnp.transpose(g_parts, (2, 0, 1, 3))
    g_parts = lax.all_to_all(g_parts, "uly", 0, 0, tiled=True)
    g_split = jnp.transpose(g_parts, (1, 0, 2, 3)).reshape(head_shape)

    cumulative, last_cum, decay_mask = decay_tables(log_decay)
    rise_rows = to_rows(jnp.exp(cumulative))
    fall_rows = to_rows(jnp.exp(last_cum - cumulative))
    scaled_query = (rise_rows * q_split).astype(jnp.bfloat16)
    scaled_key = (fall_rows * k_split).astype(jnp.bfloat16)
    update = jnp.einsum("bjhd,bjhe->bhde", scaled_key, v_split, preferred_element_type=jnp.float32)

    last_all = lax.all_gather(last_cum[..., 0], "ctx")
    forward_w, backward_w = block_weights(last_all)
    local_grad = jnp.einsum(
        "bihd,bihe->bhde", scaled_query, g_split, preferred_element_type=jnp.float32
    )
    send = jnp.stack([to_pieces(update, ctx_count), to_pieces(local_grad, ctx_count)], axis=1)
    got = lax.all_to_all(send.astype(jnp.bfloat16), "ctx", 0, 0, tiled=True)
    mixed = jnp.stack(
        [mix_blocks(forward_w, got[:, 0]), mix_blocks(backward_w, got[:, 1])], axis=1
    ).astype(jnp.bfloat16)
    back = lax.all_to_all(mixed, "ctx", 0, 0, tiled=True)
    state_b = from_pieces(back[:, 0])
    carried_b = from_pieces(back[:, 1])

    scores = jnp.einsum("bihd,bjhd->bhij", q_split, k_split, preferred_element_type=jnp.float32)
    attn_weights = (scores * decay_mask).astype(jnp.bfloat16)
    grad_raw = jnp.einsum("bihe,bjhe->bhij", g_split, v_split, preferred_element_type=jnp.float32)
    grad_scores = (grad_raw * decay_mask).astype(jnp.bfloat16)
    attended = jnp.einsum(
        "bhij,bjhd->bihd", attn_weights, v_split, preferred_element_type=jnp.float32
    )
    attended = attended + jnp.einsum(
        "bihd,bhde->bihe", scaled_query, state_b, preferred_element_type=jnp.float32
    )
    query_part = jnp.einsum(
        "bhij,bjhd->bihd", grad_scores, k_split, preferred_element_type=jnp.float32
    )
    query_part = query_part + rise_rows * jnp.einsum(
        "bihe,bhde->bihd", g_split, state_b, preferred_element_type=jnp.float32
    )
    key_part = jnp.einsum(
        "bhij,bihd->bjhd", grad_scores, q_split, preferred_element_type=jnp.float32
    )
    key_part = key_part + fall_rows * jnp.einsum(
        "bjhe,bhde->bjhd", v_split, carried_b, preferred_element_type=jnp.float32
    )
    value_part = jnp.einsum(
        "bhij,bihe->bjhe", attn_weights, g_split, preferred_element_type=jnp.float32
    )
    value_part = value_part + fall_rows * jnp.einsum(
        "bjhd,bhde->bjhe", k_split, carried_b, preferred_element_type=jnp.float32
    )

    outs = jnp.stack([attended, query_part, key_part, value_part]).astype(jnp.bfloat16)
    outs = outs.reshape(4, batch_count, uly_count, positions // uly_count, width_heads)
    outs = jnp.transpose(outs, (2, 0, 1, 3, 4))
    outs = lax.all_to_all(outs, "uly", 0, 0, tiled=True)
    outs = jnp.transpose(outs, (1, 2, 3, 0, 4)).reshape(
        4, batch_count, positions // uly_count, uly_count * width_heads
    )
    return (outs[0], outs[1], outs[2], outs[3])


def solution(mesh):
    placed = (
        P(None, "ctx", "uly"),
        P(None, "ctx", "uly"),
        P(None, "ctx", "uly"),
        P(None, ("ctx", "uly"), None),
        P(None, "uly", "ctx"),
    )
    return jax.shard_map(
        local,
        mesh=mesh,
        in_specs=placed,
        out_specs=(
            P(None, ("ctx", "uly"), None),
            P(None, ("ctx", "uly"), None),
            P(None, ("ctx", "uly"), None),
            P(None, ("ctx", "uly"), None),
        ),
        check_vma=False,
    )
```

```python
import jax
import jax.numpy as jnp
from jax import lax
from jax.sharding import PartitionSpec as P


def decay_tables(log_decay):
    cumulative = jnp.cumsum(log_decay, axis=-1)
    last_cum = cumulative[..., -1:]
    block_len = log_decay.shape[-1]
    row_ids = lax.broadcasted_iota(jnp.int32, (block_len, block_len), 0)
    col_ids = lax.broadcasted_iota(jnp.int32, (block_len, block_len), 1)
    lower_tri = row_ids >= col_ids
    spread = cumulative[..., :, None] - cumulative[..., None, :]
    decay_mask = jnp.where(lower_tri, jnp.exp(jnp.where(lower_tri, spread, 0.0)), 0.0)
    return (cumulative, last_cum, decay_mask)


def to_rows(table):
    return jnp.swapaxes(table, 1, 2)[..., None]


def to_pieces(state, count):
    batch_count, head_count, width, _ = state.shape
    banded = state.reshape(batch_count, head_count, count, width // count, width)
    return jnp.transpose(banded, (2, 0, 1, 3, 4))


def from_pieces(pieces):
    count, batch_count, head_count, rows, width = pieces.shape
    return jnp.transpose(pieces, (1, 2, 0, 3, 4)).reshape(batch_count, head_count, count * rows, width)


def block_weights(last_all):
    count = last_all.shape[0]
    inclusive = jnp.cumsum(last_all, axis=0)
    exclusive = inclusive - last_all
    inc = jnp.transpose(inclusive, (1, 2, 0))
    exc = jnp.transpose(exclusive, (1, 2, 0))
    row_ids = lax.broadcasted_iota(jnp.int32, (count, count), 0)
    col_ids = lax.broadcasted_iota(jnp.int32, (count, count), 1)
    earlier = col_ids < row_ids
    later = col_ids > row_ids
    forward_gap = exc[..., :, None] - inc[..., None, :]
    backward_gap = exc[..., None, :] - inc[..., :, None]
    forward = jnp.where(earlier, jnp.exp(jnp.where(earlier, forward_gap, 0.0)), 0.0)
    backward = jnp.where(later, jnp.exp(jnp.where(later, backward_gap, 0.0)), 0.0)
    return forward, backward


def mix_blocks(weights, pieces):
    return jnp.einsum(
        "bhcd,dbhrx->cbhrx", weights, pieces, precision=lax.Precision.HIGHEST,
        preferred_element_type=jnp.float32,
    )


def local(query_heads, key_heads, value_heads, grad_out, log_decay):
    batch_count, positions, width_heads = query_heads.shape
    head_count = log_decay.shape[1]
    width = width_heads // head_count
    uly_count = lax.axis_size("uly")
    ctx_count = lax.axis_size("ctx")
    head_shape = (batch_count, positions, head_count, width)
    q_split = query_heads.reshape(head_shape)
    k_split = key_heads.reshape(head_shape)
    v_split = value_heads.reshape(head_shape)

    rows_in = grad_out.shape[1]
    g_parts = grad_out.reshape(batch_count, rows_in, uly_count, width_heads)
    g_parts = jnp.transpose(g_parts, (2, 0, 1, 3))
    g_parts = lax.all_to_all(g_parts, "uly", 0, 0, tiled=True)
    g_split = jnp.transpose(g_parts, (1, 0, 2, 3)).reshape(head_shape)

    cumulative, last_cum, decay_mask = decay_tables(log_decay)
    rise_rows = to_rows(jnp.exp(cumulative))
    fall_rows = to_rows(jnp.exp(last_cum - cumulative))
    scaled_query = (rise_rows * q_split).astype(jnp.bfloat16)
    scaled_key = (fall_rows * k_split).astype(jnp.bfloat16)
    update = jnp.einsum("bjhd,bjhe->bhde", scaled_key, v_split, preferred_element_type=jnp.float32)

    local_grad = jnp.einsum(
        "bihd,bihe->bhde", scaled_query, g_split, preferred_element_type=jnp.float32
    )
    band = width // ctx_count
    last_row = jnp.broadcast_to(last_cum, (batch_count, head_count, width))
    last_piece = jnp.broadcast_to(last_row[None, :, :, None, :], (ctx_count, batch_count, head_count, 1, width))
    send = jnp.concatenate(
        [to_pieces(update, ctx_count), to_pieces(local_grad, ctx_count), last_piece], axis=3
    )
    got = lax.all_to_all(send, "ctx", 0, 0, tiled=True)
    forward_w, backward_w = block_weights(got[:, :, :, 2 * band, 0])
    mixed = jnp.stack(
        [
            mix_blocks(forward_w, got[:, :, :, :band]),
            mix_blocks(backward_w, got[:, :, :, band : 2 * band]),
        ],
        axis=1,
    ).astype(jnp.bfloat16)
    back = lax.all_to_all(mixed, "ctx", 0, 0, tiled=True)
    state_b = from_pieces(back[:, 0])
    carried_b = from_pieces(back[:, 1])

    scores = jnp.einsum("bihd,bjhd->bhij", q_split, k_split, preferred_element_type=jnp.float32)
    attn_weights = (scores * decay_mask).astype(jnp.bfloat16)
    grad_raw = jnp.einsum("bihe,bjhe->bhij", g_split, v_split, preferred_element_type=jnp.float32)
    grad_scores = (grad_raw * decay_mask).astype(jnp.bfloat16)
    attended = jnp.einsum(
        "bhij,bjhd->bihd", attn_weights, v_split, preferred_element_type=jnp.float32
    )
    attended = attended + jnp.einsum(
        "bihd,bhde->bihe", scaled_query, state_b, preferred_element_type=jnp.float32
    )
    query_part = jnp.einsum(
        "bhij,bjhd->bihd", grad_scores, k_split, preferred_element_type=jnp.float32
    )
    query_part = query_part + rise_rows * jnp.einsum(
        "bihe,bhde->bihd", g_split, state_b, preferred_element_type=jnp.float32
    )
    key_part = jnp.einsum(
        "bhij,bihd->bjhd", grad_scores, q_split, preferred_element_type=jnp.float32
    )
    key_part = key_part + fall_rows * jnp.einsum(
        "bjhe,bhde->bjhd", v_split, carried_b, preferred_element_type=jnp.float32
    )
    value_part = jnp.einsum(
        "bhij,bihe->bjhe", attn_weights, g_split, preferred_element_type=jnp.float32
    )
    value_part = value_part + fall_rows * jnp.einsum(
        "bjhd,bhde->bjhe", k_split, carried_b, preferred_element_type=jnp.float32
    )

    outs = jnp.stack([attended, query_part, key_part, value_part]).astype(jnp.bfloat16)
    outs = outs.reshape(4, batch_count, uly_count, positions // uly_count, width_heads)
    outs = jnp.transpose(outs, (2, 0, 1, 3, 4))
    outs = lax.all_to_all(outs, "uly", 0, 0, tiled=True)
    outs = jnp.transpose(outs, (1, 2, 3, 0, 4)).reshape(
        4, batch_count, positions // uly_count, uly_count * width_heads
    )
    return (outs[0], outs[1], outs[2], outs[3])


def solution(mesh):
    placed = (
        P(None, "ctx", "uly"),
        P(None, "ctx", "uly"),
        P(None, "ctx", "uly"),
        P(None, ("ctx", "uly"), None),
        P(None, "uly", "ctx"),
    )
    return jax.shard_map(
        local,
        mesh=mesh,
        in_specs=placed,
        out_specs=(
            P(None, ("ctx", "uly"), None),
            P(None, ("ctx", "uly"), None),
            P(None, ("ctx", "uly"), None),
            P(None, ("ctx", "uly"), None),
        ),
        check_vma=False,
    )
```

```python
import jax
import jax.numpy as jnp
from jax import lax
from jax.sharding import Mesh, PartitionSpec as P


def decay_tables(log_decay):
    cumulative = jnp.cumsum(log_decay, axis=-1)
    last_cum = cumulative[..., -1:]
    block_len = log_decay.shape[-1]
    row_ids = lax.broadcasted_iota(jnp.int32, (block_len, block_len), 0)
    col_ids = lax.broadcasted_iota(jnp.int32, (block_len, block_len), 1)
    lower_tri = row_ids >= col_ids
    spread = cumulative[..., :, None] - cumulative[..., None, :]
    decay_mask = jnp.where(lower_tri, jnp.exp(jnp.where(lower_tri, spread, 0.0)), 0.0)
    return (cumulative, last_cum, decay_mask)


def to_rows(table):
    return jnp.swapaxes(table, 1, 2)[..., None]


def to_pieces(state, count):
    batch_count, head_count, rows, width = state.shape
    banded = state.reshape(batch_count, head_count, count, rows // count, width)
    return jnp.transpose(banded, (2, 0, 1, 3, 4))


def from_pieces(pieces):
    count, batch_count, head_count, rows, width = pieces.shape
    return jnp.transpose(pieces, (1, 2, 0, 3, 4)).reshape(batch_count, head_count, count * rows, width)


def block_weights(last_all):
    count = last_all.shape[0]
    inclusive = jnp.cumsum(last_all, axis=0)
    exclusive = inclusive - last_all
    inc = jnp.transpose(inclusive, (1, 2, 0))
    exc = jnp.transpose(exclusive, (1, 2, 0))
    row_ids = lax.broadcasted_iota(jnp.int32, (count, count), 0)
    col_ids = lax.broadcasted_iota(jnp.int32, (count, count), 1)
    earlier = col_ids < row_ids
    later = col_ids > row_ids
    forward_gap = exc[..., :, None] - inc[..., None, :]
    backward_gap = exc[..., None, :] - inc[..., :, None]
    forward = jnp.where(earlier, jnp.exp(jnp.where(earlier, forward_gap, 0.0)), 0.0)
    backward = jnp.where(later, jnp.exp(jnp.where(later, backward_gap, 0.0)), 0.0)
    return forward, backward


def mix_blocks(weights, pieces):
    return jnp.einsum(
        "bhcd,dbhrx->cbhrx", weights, pieces, precision=lax.Precision.HIGHEST,
        preferred_element_type=jnp.float32,
    )


def local(query_heads, key_heads, value_heads, grad_out, log_decay):
    batch_count, positions, width_heads = query_heads.shape
    head_count = log_decay.shape[1]
    width = width_heads // head_count
    uly_count = lax.axis_size("uly")
    head_shape = (batch_count, positions, head_count, width)
    q_split = query_heads.reshape(head_shape)
    k_split = key_heads.reshape(head_shape)
    v_split = value_heads.reshape(head_shape)

    rows_in = grad_out.shape[1]
    g_parts = grad_out.reshape(batch_count, rows_in, uly_count, width_heads)
    g_parts = jnp.transpose(g_parts, (2, 0, 1, 3))
    g_parts = lax.all_to_all(g_parts, "uly", 0, 0, tiled=True)
    g_split = jnp.transpose(g_parts, (1, 0, 2, 3)).reshape(head_shape)

    cumulative, last_cum, decay_mask = decay_tables(log_decay)
    rise_rows = to_rows(jnp.exp(cumulative))
    fall_rows = to_rows(jnp.exp(last_cum - cumulative))
    scaled_query = (rise_rows * q_split).astype(jnp.bfloat16)
    scaled_key = (fall_rows * k_split).astype(jnp.bfloat16)
    update = jnp.einsum("bjhd,bjhe->bhde", scaled_key, v_split, preferred_element_type=jnp.float32)

    local_grad = jnp.einsum(
        "bihd,bihe->bhde", scaled_query, g_split, preferred_element_type=jnp.float32
    )
    chip_count = lax.axis_size("z")
    core = lax.axis_index("core")
    second = core == 1
    pairs = [(0, 1), (1, 0)]
    last = last_cum[..., 0]
    other_update, other_grad, other_last = lax.ppermute((update, local_grad, last), "core", pairs)

    def order(mine, other):
        return jnp.where(second, other, mine), jnp.where(second, mine, other)

    update_lo, update_hi = order(update, other_update)
    grad_lo, grad_hi = order(local_grad, other_grad)
    last_lo, last_hi = order(last, other_last)
    keep_lo = jnp.exp(last_lo)[..., None, None]
    keep_hi = jnp.exp(last_hi)[..., None, None]
    chip_update = keep_hi * update_lo + update_hi
    chip_grad = keep_lo * grad_hi + grad_lo
    half = width // 2
    band = half // chip_count

    def my_half(state):
        return lax.dynamic_slice_in_dim(state, core * half, half, axis=2)

    chip_last = jnp.broadcast_to((last_lo + last_hi)[..., None], (batch_count, head_count, width))
    last_piece = jnp.broadcast_to(
        chip_last[None, :, :, None, :], (chip_count, batch_count, head_count, 1, width)
    )
    send = jnp.concatenate(
        [to_pieces(my_half(chip_update), chip_count), to_pieces(my_half(chip_grad), chip_count), last_piece],
        axis=3,
    )
    got = lax.all_to_all(send, "z", 0, 0, tiled=True)
    forward_w, backward_w = block_weights(got[:, :, :, 2 * band, 0])
    mixed = jnp.stack(
        [
            mix_blocks(forward_w, got[:, :, :, :band]),
            mix_blocks(backward_w, got[:, :, :, band : 2 * band]),
        ],
        axis=1,
    )
    back = lax.all_to_all(mixed, "z", 0, 0, tiled=True)
    halves = jnp.stack([from_pieces(back[:, 0]), from_pieces(back[:, 1])])
    other_halves = lax.ppermute(halves, "core", pairs)
    low_rows, high_rows = order(halves, other_halves)
    entering = jnp.concatenate([low_rows, high_rows], axis=3)
    state_b = jnp.where(second, keep_lo * entering[0] + update_lo, entering[0]).astype(jnp.bfloat16)
    carried_b = jnp.where(second, entering[1], keep_hi * entering[1] + grad_hi).astype(jnp.bfloat16)

    scores = jnp.einsum("bihd,bjhd->bhij", q_split, k_split, preferred_element_type=jnp.float32)
    attn_weights = (scores * decay_mask).astype(jnp.bfloat16)
    grad_raw = jnp.einsum("bihe,bjhe->bhij", g_split, v_split, preferred_element_type=jnp.float32)
    grad_scores = (grad_raw * decay_mask).astype(jnp.bfloat16)
    attended = jnp.einsum(
        "bhij,bjhd->bihd", attn_weights, v_split, preferred_element_type=jnp.float32
    )
    attended = attended + jnp.einsum(
        "bihd,bhde->bihe", scaled_query, state_b, preferred_element_type=jnp.float32
    )
    query_part = jnp.einsum(
        "bhij,bjhd->bihd", grad_scores, k_split, preferred_element_type=jnp.float32
    )
    query_part = query_part + rise_rows * jnp.einsum(
        "bihe,bhde->bihd", g_split, state_b, preferred_element_type=jnp.float32
    )
    key_part = jnp.einsum(
        "bhij,bihd->bjhd", grad_scores, q_split, preferred_element_type=jnp.float32
    )
    key_part = key_part + fall_rows * jnp.einsum(
        "bjhe,bhde->bjhd", v_split, carried_b, preferred_element_type=jnp.float32
    )
    value_part = jnp.einsum(
        "bhij,bihe->bjhe", attn_weights, g_split, preferred_element_type=jnp.float32
    )
    value_part = value_part + fall_rows * jnp.einsum(
        "bjhd,bhde->bjhe", k_split, carried_b, preferred_element_type=jnp.float32
    )

    outs = jnp.stack([attended, query_part, key_part, value_part]).astype(jnp.bfloat16)
    outs = outs.reshape(4, batch_count, uly_count, positions // uly_count, width_heads)
    outs = jnp.transpose(outs, (2, 0, 1, 3, 4))
    outs = lax.all_to_all(outs, "uly", 0, 0, tiled=True)
    outs = jnp.transpose(outs, (1, 2, 3, 0, 4)).reshape(
        4, batch_count, positions // uly_count, uly_count * width_heads
    )
    return (outs[0], outs[1], outs[2], outs[3])


def solution(mesh):
    ctx_count, uly_count = mesh.shape["ctx"], mesh.shape["uly"]
    grid = mesh.devices.reshape(ctx_count // 2, 2, uly_count)
    chips = Mesh(grid, ("z", "core", "uly"))
    placed = (
        P(None, ("z", "core"), "uly"),
        P(None, ("z", "core"), "uly"),
        P(None, ("z", "core"), "uly"),
        P(None, ("z", "core", "uly"), None),
        P(None, "uly", ("z", "core")),
    )
    return jax.shard_map(
        local,
        mesh=chips,
        in_specs=placed,
        out_specs=(
            P(None, ("z", "core", "uly"), None),
            P(None, ("z", "core", "uly"), None),
            P(None, ("z", "core", "uly"), None),
            P(None, ("z", "core", "uly"), None),
        ),
        check_vma=False,
    )
```

```python
import jax
import jax.numpy as jnp
from jax import lax
from jax.sharding import Mesh, PartitionSpec as P


def decay_tables(log_decay):
    cumulative = jnp.cumsum(log_decay, axis=-1)
    last_cum = cumulative[..., -1:]
    block_len = log_decay.shape[-1]
    row_ids = lax.broadcasted_iota(jnp.int32, (block_len, block_len), 0)
    col_ids = lax.broadcasted_iota(jnp.int32, (block_len, block_len), 1)
    lower_tri = row_ids >= col_ids
    spread = cumulative[..., :, None] - cumulative[..., None, :]
    decay_mask = jnp.where(lower_tri, jnp.exp(jnp.where(lower_tri, spread, 0.0)), 0.0)
    return (cumulative, last_cum, decay_mask)


def to_rows(table):
    return jnp.swapaxes(table, 1, 2)[..., None]


def to_pieces(state, count):
    batch_count, head_count, rows, width = state.shape
    banded = state.reshape(batch_count, head_count, count, rows // count, width)
    return jnp.transpose(banded, (2, 0, 1, 3, 4))


def from_pieces(pieces):
    count, batch_count, head_count, rows, width = pieces.shape
    return jnp.transpose(pieces, (1, 2, 0, 3, 4)).reshape(batch_count, head_count, count * rows, width)


def block_weights(last_all):
    count = last_all.shape[0]
    inclusive = jnp.cumsum(last_all, axis=0)
    exclusive = inclusive - last_all
    inc = jnp.transpose(inclusive, (1, 2, 0))
    exc = jnp.transpose(exclusive, (1, 2, 0))
    row_ids = lax.broadcasted_iota(jnp.int32, (count, count), 0)
    col_ids = lax.broadcasted_iota(jnp.int32, (count, count), 1)
    earlier = col_ids < row_ids
    later = col_ids > row_ids
    forward_gap = exc[..., :, None] - inc[..., None, :]
    backward_gap = exc[..., None, :] - inc[..., :, None]
    forward = jnp.where(earlier, jnp.exp(jnp.where(earlier, forward_gap, 0.0)), 0.0)
    backward = jnp.where(later, jnp.exp(jnp.where(later, backward_gap, 0.0)), 0.0)
    return forward, backward


def mix_blocks(weights, pieces):
    return jnp.einsum(
        "bhcd,dbhrx->cbhrx", weights, pieces, precision=lax.Precision.HIGHEST,
        preferred_element_type=jnp.float32,
    )


def local(query_heads, key_heads, value_heads, grad_out, log_decay):
    batch_count, positions, width_heads = query_heads.shape
    head_count = log_decay.shape[1]
    width = width_heads // head_count
    uly_count = lax.axis_size("uly")
    head_shape = (batch_count, positions, head_count, width)
    q_split = query_heads.reshape(head_shape)
    k_split = key_heads.reshape(head_shape)
    v_split = value_heads.reshape(head_shape)

    rows_in = grad_out.shape[1]
    g_parts = grad_out.reshape(batch_count, rows_in, uly_count, width_heads)
    g_parts = jnp.transpose(g_parts, (2, 0, 1, 3))
    g_parts = lax.all_to_all(g_parts, "uly", 0, 0, tiled=True)
    g_split = jnp.transpose(g_parts, (1, 0, 2, 3)).reshape(head_shape)

    cumulative, last_cum, decay_mask = decay_tables(log_decay)
    rise_rows = to_rows(jnp.exp(cumulative))
    fall_rows = to_rows(jnp.exp(last_cum - cumulative))
    scaled_query = (rise_rows * q_split).astype(jnp.bfloat16)
    scaled_key = (fall_rows * k_split).astype(jnp.bfloat16)
    update = jnp.einsum("bjhd,bjhe->bhde", scaled_key, v_split, preferred_element_type=jnp.float32)

    local_grad = jnp.einsum(
        "bihd,bihe->bhde", scaled_query, g_split, preferred_element_type=jnp.float32
    )
    chip_count = lax.axis_size("z")
    core = lax.axis_index("core")
    second = core == 1
    pairs = [(0, 1), (1, 0)]
    last = last_cum[..., 0]
    other_update, other_grad, other_last = lax.ppermute((update, local_grad, last), "core", pairs)

    def order(mine, other):
        return jnp.where(second, other, mine), jnp.where(second, mine, other)

    update_lo, update_hi = order(update, other_update)
    grad_lo, grad_hi = order(local_grad, other_grad)
    last_lo, last_hi = order(last, other_last)
    keep_lo = jnp.exp(last_lo)[..., None, None]
    keep_hi = jnp.exp(last_hi)[..., None, None]
    chip_update = keep_hi * update_lo + update_hi
    chip_grad = keep_lo * grad_hi + grad_lo
    half = width // 2
    band = half // chip_count

    def my_half(state):
        return lax.dynamic_slice_in_dim(state, core * half, half, axis=2)

    chip_last = (last_lo + last_hi).reshape(1, batch_count * head_count)
    chip_last = jnp.pad(chip_last, ((0, 0), (0, width - batch_count * head_count)))
    last_piece = jnp.broadcast_to(chip_last, (chip_count, width))
    sent = jnp.concatenate(
        [to_pieces(my_half(chip_update), chip_count), to_pieces(my_half(chip_grad), chip_count)], axis=3
    )
    piece_shape = sent.shape
    send = jnp.concatenate([sent.reshape(chip_count, -1), last_piece], axis=1)
    got = lax.all_to_all(send, "z", 0, 0, tiled=True)
    got_last = got[:, -width:][:, : batch_count * head_count].reshape(chip_count, batch_count, head_count)
    got = got[:, :-width].reshape(piece_shape)
    forward_w, backward_w = block_weights(got_last)
    mixed = jnp.stack(
        [
            mix_blocks(forward_w, got[:, :, :, :band]),
            mix_blocks(backward_w, got[:, :, :, band : 2 * band]),
        ],
        axis=1,
    )
    back = lax.all_to_all(mixed, "z", 0, 0, tiled=True)
    halves = jnp.stack([from_pieces(back[:, 0]), from_pieces(back[:, 1])])
    other_halves = lax.ppermute(halves, "core", pairs)
    low_rows, high_rows = order(halves, other_halves)
    entering = jnp.concatenate([low_rows, high_rows], axis=3)
    state_b = jnp.where(second, keep_lo * entering[0] + update_lo, entering[0]).astype(jnp.bfloat16)
    carried_b = jnp.where(second, entering[1], keep_hi * entering[1] + grad_hi).astype(jnp.bfloat16)

    scores = jnp.einsum("bihd,bjhd->bhij", q_split, k_split, preferred_element_type=jnp.float32)
    attn_weights = (scores * decay_mask).astype(jnp.bfloat16)
    grad_raw = jnp.einsum("bihe,bjhe->bhij", g_split, v_split, preferred_element_type=jnp.float32)
    grad_scores = (grad_raw * decay_mask).astype(jnp.bfloat16)
    attended = jnp.einsum(
        "bhij,bjhd->bihd", attn_weights, v_split, preferred_element_type=jnp.float32
    )
    attended = attended + jnp.einsum(
        "bihd,bhde->bihe", scaled_query, state_b, preferred_element_type=jnp.float32
    )
    query_part = jnp.einsum(
        "bhij,bjhd->bihd", grad_scores, k_split, preferred_element_type=jnp.float32
    )
    query_part = query_part + rise_rows * jnp.einsum(
        "bihe,bhde->bihd", g_split, state_b, preferred_element_type=jnp.float32
    )
    key_part = jnp.einsum(
        "bhij,bihd->bjhd", grad_scores, q_split, preferred_element_type=jnp.float32
    )
    key_part = key_part + fall_rows * jnp.einsum(
        "bjhe,bhde->bjhd", v_split, carried_b, preferred_element_type=jnp.float32
    )
    value_part = jnp.einsum(
        "bhij,bihe->bjhe", attn_weights, g_split, preferred_element_type=jnp.float32
    )
    value_part = value_part + fall_rows * jnp.einsum(
        "bjhd,bhde->bjhe", k_split, carried_b, preferred_element_type=jnp.float32
    )

    outs = jnp.stack([attended, query_part, key_part, value_part]).astype(jnp.bfloat16)
    outs = outs.reshape(4, batch_count, uly_count, positions // uly_count, width_heads)
    outs = jnp.transpose(outs, (2, 0, 1, 3, 4))
    outs = lax.all_to_all(outs, "uly", 0, 0, tiled=True)

    def to_tokens(index):
        return jnp.transpose(outs[:, index], (1, 2, 0, 3)).reshape(
            batch_count, positions // uly_count, uly_count * width_heads
        )

    return (to_tokens(0), to_tokens(1), to_tokens(2), to_tokens(3))


def solution(mesh):
    ctx_count, uly_count = mesh.shape["ctx"], mesh.shape["uly"]
    grid = mesh.devices.reshape(ctx_count // 2, 2, uly_count)
    chips = Mesh(grid, ("z", "core", "uly"))
    placed = (
        P(None, ("z", "core"), "uly"),
        P(None, ("z", "core"), "uly"),
        P(None, ("z", "core"), "uly"),
        P(None, ("z", "core", "uly"), None),
        P(None, "uly", ("z", "core")),
    )
    return jax.shard_map(
        local,
        mesh=chips,
        in_specs=placed,
        out_specs=(
            P(None, ("z", "core", "uly"), None),
            P(None, ("z", "core", "uly"), None),
            P(None, ("z", "core", "uly"), None),
            P(None, ("z", "core", "uly"), None),
        ),
        check_vma=False,
    )
```

```python
import jax
import jax.numpy as jnp
from jax import lax
from jax.sharding import Mesh, PartitionSpec as P


def decay_tables(log_decay):
    cumulative = jnp.cumsum(log_decay, axis=-1)
    last_cum = cumulative[..., -1:]
    block_len = log_decay.shape[-1]
    row_ids = lax.broadcasted_iota(jnp.int32, (block_len, block_len), 0)
    col_ids = lax.broadcasted_iota(jnp.int32, (block_len, block_len), 1)
    lower_tri = row_ids >= col_ids
    spread = cumulative[..., :, None] - cumulative[..., None, :]
    decay_mask = jnp.where(lower_tri, jnp.exp(jnp.where(lower_tri, spread, 0.0)), 0.0)
    return (cumulative, last_cum, decay_mask)


def to_rows(table):
    return jnp.swapaxes(table, 1, 2)[..., None]


def to_pieces(state, count):
    batch_count, head_count, rows, width = state.shape
    banded = state.reshape(batch_count, head_count, count, rows // count, width)
    return jnp.transpose(banded, (2, 0, 1, 3, 4))


def from_pieces(pieces):
    count, batch_count, head_count, rows, width = pieces.shape
    return jnp.transpose(pieces, (1, 2, 0, 3, 4)).reshape(batch_count, head_count, count * rows, width)


def block_weights(last_all):
    count = last_all.shape[0]
    inclusive = jnp.cumsum(last_all, axis=0)
    exclusive = inclusive - last_all
    inc = jnp.transpose(inclusive, (1, 2, 0))
    exc = jnp.transpose(exclusive, (1, 2, 0))
    row_ids = lax.broadcasted_iota(jnp.int32, (count, count), 0)
    col_ids = lax.broadcasted_iota(jnp.int32, (count, count), 1)
    earlier = col_ids < row_ids
    later = col_ids > row_ids
    forward_gap = exc[..., :, None] - inc[..., None, :]
    backward_gap = exc[..., None, :] - inc[..., :, None]
    forward = jnp.where(earlier, jnp.exp(jnp.where(earlier, forward_gap, 0.0)), 0.0)
    backward = jnp.where(later, jnp.exp(jnp.where(later, backward_gap, 0.0)), 0.0)
    return forward, backward


def mix_blocks(weights, pieces):
    return jnp.einsum(
        "bhcd,dbhrx->cbhrx", weights, pieces, precision=lax.Precision.HIGHEST,
        preferred_element_type=jnp.float32,
    )


def local(query_heads, key_heads, value_heads, grad_out, log_decay):
    batch_count, positions, width_heads = query_heads.shape
    head_count = log_decay.shape[1]
    width = width_heads // head_count
    uly_count = lax.axis_size("uly")
    head_shape = (batch_count, positions, head_count, width)
    q_split = query_heads.reshape(head_shape)
    k_split = key_heads.reshape(head_shape)
    v_split = value_heads.reshape(head_shape)

    rows_in = grad_out.shape[1]
    g_parts = grad_out.reshape(batch_count, rows_in, uly_count, width_heads)
    g_parts = jnp.transpose(g_parts, (2, 0, 1, 3))
    g_parts = lax.all_to_all(g_parts, "uly", 0, 0, tiled=True)
    g_split = jnp.transpose(g_parts, (1, 0, 2, 3)).reshape(head_shape)

    cumulative, last_cum, decay_mask = decay_tables(log_decay)
    rise_rows = to_rows(jnp.exp(cumulative))
    fall_rows = to_rows(jnp.exp(last_cum - cumulative))
    scaled_query = (rise_rows * q_split).astype(jnp.bfloat16)
    scaled_key = (fall_rows * k_split).astype(jnp.bfloat16)
    update = jnp.einsum("bjhd,bjhe->bhde", scaled_key, v_split, preferred_element_type=jnp.float32)

    local_grad = jnp.einsum(
        "bihd,bihe->bhde", scaled_query, g_split, preferred_element_type=jnp.float32
    )
    group_count = lax.axis_size("zg")
    inner_count = lax.axis_size("zl")
    core = lax.axis_index("core")
    second = core == 1
    pairs = [(0, 1), (1, 0)]
    last = last_cum[..., 0]
    other_update, other_grad, other_last = lax.ppermute((update, local_grad, last), "core", pairs)

    def order(mine, other):
        return jnp.where(second, other, mine), jnp.where(second, mine, other)

    update_lo, update_hi = order(update, other_update)
    grad_lo, grad_hi = order(local_grad, other_grad)
    last_lo, last_hi = order(last, other_last)
    keep_lo = jnp.exp(last_lo)[..., None, None]
    keep_hi = jnp.exp(last_hi)[..., None, None]
    chip_update = keep_hi * update_lo + update_hi
    chip_grad = keep_lo * grad_hi + grad_lo
    half = width // 2
    band = half // inner_count

    def my_half(state):
        return lax.dynamic_slice_in_dim(state, core * half, half, axis=2)

    chip_last = jnp.broadcast_to((last_lo + last_hi)[..., None], (batch_count, head_count, width))
    last_piece = jnp.broadcast_to(
        chip_last[None, :, :, None, :], (inner_count, batch_count, head_count, 1, width)
    )
    send = jnp.concatenate(
        [to_pieces(my_half(chip_update), inner_count), to_pieces(my_half(chip_grad), inner_count), last_piece],
        axis=3,
    )
    got = lax.all_to_all(send, "zl", 0, 0, tiled=True)
    chip_states = got[:, :, :, :band]
    chip_grads = got[:, :, :, band : 2 * band]
    chip_lasts = got[:, :, :, 2 * band, 0]
    forward_w, backward_w = block_weights(chip_lasts)
    within_state = mix_blocks(forward_w, chip_states)
    within_grad = mix_blocks(backward_w, chip_grads)
    inclusive = jnp.cumsum(chip_lasts, axis=0)
    exclusive = inclusive - chip_lasts
    total = inclusive[-1]
    after_rise = jnp.exp(total[None] - inclusive)[..., None, None]
    before_rise = jnp.exp(exclusive)[..., None, None]
    group_state = jnp.sum(after_rise * chip_states, axis=0)
    group_grad = jnp.sum(before_rise * chip_grads, axis=0)
    group_keep = jnp.exp(total)[..., None, None]
    upward = [(index, index + 1) for index in range(group_count - 1)]
    downward = [(index + 1, index) for index in range(group_count - 1)]
    entering_group = jnp.zeros_like(group_state)
    leaving_group = jnp.zeros_like(group_grad)
    for _ in range(group_count - 1):
        entering_group, leaving_group = (
            lax.ppermute(group_keep * entering_group + group_state, "zg", upward),
            lax.ppermute(group_keep * leaving_group + group_grad, "zg", downward),
        )
    state_pieces = within_state + before_rise * entering_group[None]
    grad_pieces = within_grad + after_rise * leaving_group[None]
    mixed = jnp.stack([state_pieces, grad_pieces], axis=1)
    back = lax.all_to_all(mixed, "zl", 0, 0, tiled=True)
    halves = jnp.stack([from_pieces(back[:, 0]), from_pieces(back[:, 1])])
    other_halves = lax.ppermute(halves, "core", pairs)
    low_rows, high_rows = order(halves, other_halves)
    entering = jnp.concatenate([low_rows, high_rows], axis=3)
    state_b = jnp.where(second, keep_lo * entering[0] + update_lo, entering[0]).astype(jnp.bfloat16)
    carried_b = jnp.where(second, entering[1], keep_hi * entering[1] + grad_hi).astype(jnp.bfloat16)

    scores = jnp.einsum("bihd,bjhd->bhij", q_split, k_split, preferred_element_type=jnp.float32)
    attn_weights = (scores * decay_mask).astype(jnp.bfloat16)
    grad_raw = jnp.einsum("bihe,bjhe->bhij", g_split, v_split, preferred_element_type=jnp.float32)
    grad_scores = (grad_raw * decay_mask).astype(jnp.bfloat16)
    attended = jnp.einsum(
        "bhij,bjhd->bihd", attn_weights, v_split, preferred_element_type=jnp.float32
    )
    attended = attended + jnp.einsum(
        "bihd,bhde->bihe", scaled_query, state_b, preferred_element_type=jnp.float32
    )
    query_part = jnp.einsum(
        "bhij,bjhd->bihd", grad_scores, k_split, preferred_element_type=jnp.float32
    )
    query_part = query_part + rise_rows * jnp.einsum(
        "bihe,bhde->bihd", g_split, state_b, preferred_element_type=jnp.float32
    )
    key_part = jnp.einsum(
        "bhij,bihd->bjhd", grad_scores, q_split, preferred_element_type=jnp.float32
    )
    key_part = key_part + fall_rows * jnp.einsum(
        "bjhe,bhde->bjhd", v_split, carried_b, preferred_element_type=jnp.float32
    )
    value_part = jnp.einsum(
        "bhij,bihe->bjhe", attn_weights, g_split, preferred_element_type=jnp.float32
    )
    value_part = value_part + fall_rows * jnp.einsum(
        "bjhd,bhde->bjhe", k_split, carried_b, preferred_element_type=jnp.float32
    )

    outs = jnp.stack([attended, query_part, key_part, value_part]).astype(jnp.bfloat16)
    outs = outs.reshape(4, batch_count, uly_count, positions // uly_count, width_heads)
    outs = jnp.transpose(outs, (2, 0, 1, 3, 4))
    outs = lax.all_to_all(outs, "uly", 0, 0, tiled=True)
    outs = jnp.transpose(outs, (1, 2, 3, 0, 4)).reshape(
        4, batch_count, positions // uly_count, uly_count * width_heads
    )
    return (outs[0], outs[1], outs[2], outs[3])


def solution(mesh):
    ctx_count, uly_count = mesh.shape["ctx"], mesh.shape["uly"]
    inner = 4 if ctx_count % 8 == 0 else 1
    grid = mesh.devices.reshape(ctx_count // (2 * inner), inner, 2, uly_count)
    chips = Mesh(grid, ("zg", "zl", "core", "uly"))
    placed = (
        P(None, ("zg", "zl", "core"), "uly"),
        P(None, ("zg", "zl", "core"), "uly"),
        P(None, ("zg", "zl", "core"), "uly"),
        P(None, ("zg", "zl", "core", "uly"), None),
        P(None, "uly", ("zg", "zl", "core")),
    )
    return jax.shard_map(
        local,
        mesh=chips,
        in_specs=placed,
        out_specs=(
            P(None, ("zg", "zl", "core", "uly"), None),
            P(None, ("zg", "zl", "core", "uly"), None),
            P(None, ("zg", "zl", "core", "uly"), None),
            P(None, ("zg", "zl", "core", "uly"), None),
        ),
        check_vma=False,
    )
```

```python
import jax
import jax.numpy as jnp
from jax import lax
from jax.sharding import Mesh, PartitionSpec as P


def decay_tables(log_decay):
    cumulative = jnp.cumsum(log_decay, axis=-1)
    last_cum = cumulative[..., -1:]
    block_len = log_decay.shape[-1]
    row_ids = lax.broadcasted_iota(jnp.int32, (block_len, block_len), 0)
    col_ids = lax.broadcasted_iota(jnp.int32, (block_len, block_len), 1)
    lower_tri = row_ids >= col_ids
    spread = cumulative[..., :, None] - cumulative[..., None, :]
    decay_mask = jnp.where(lower_tri, jnp.exp(jnp.where(lower_tri, spread, 0.0)), 0.0)
    return (cumulative, last_cum, decay_mask)


def to_rows(table):
    return jnp.swapaxes(table, 1, 2)[..., None]


def to_pieces(state, count):
    batch_count, head_count, rows, width = state.shape
    banded = state.reshape(batch_count, head_count, count, rows // count, width)
    return jnp.transpose(banded, (2, 0, 1, 3, 4))


def from_pieces(pieces):
    count, batch_count, head_count, rows, width = pieces.shape
    return jnp.transpose(pieces, (1, 2, 0, 3, 4)).reshape(batch_count, head_count, count * rows, width)


def block_weights(last_all):
    count = last_all.shape[0]
    inclusive = jnp.cumsum(last_all, axis=0)
    exclusive = inclusive - last_all
    inc = jnp.transpose(inclusive, (1, 2, 0))
    exc = jnp.transpose(exclusive, (1, 2, 0))
    row_ids = lax.broadcasted_iota(jnp.int32, (count, count), 0)
    col_ids = lax.broadcasted_iota(jnp.int32, (count, count), 1)
    earlier = col_ids < row_ids
    later = col_ids > row_ids
    forward_gap = exc[..., :, None] - inc[..., None, :]
    backward_gap = exc[..., None, :] - inc[..., :, None]
    forward = jnp.where(earlier, jnp.exp(jnp.where(earlier, forward_gap, 0.0)), 0.0)
    backward = jnp.where(later, jnp.exp(jnp.where(later, backward_gap, 0.0)), 0.0)
    return forward, backward


def mix_blocks(weights, pieces):
    return jnp.einsum(
        "bhcd,dbhrx->cbhrx", weights, pieces, precision=lax.Precision.HIGHEST,
        preferred_element_type=jnp.float32,
    )


def local(query_heads, key_heads, value_heads, grad_out, log_decay):
    batch_count, positions, width_heads = query_heads.shape
    head_count = log_decay.shape[1]
    width = width_heads // head_count
    uly_count = lax.axis_size("uly")
    head_shape = (batch_count, positions, head_count, width)
    q_split = query_heads.reshape(head_shape)
    k_split = key_heads.reshape(head_shape)
    v_split = value_heads.reshape(head_shape)

    rows_in = grad_out.shape[1]
    g_parts = grad_out.reshape(batch_count, rows_in, uly_count, width_heads)
    g_parts = jnp.transpose(g_parts, (2, 0, 1, 3))
    g_parts = lax.all_to_all(g_parts, "uly", 0, 0, tiled=True)
    g_split = jnp.transpose(g_parts, (1, 0, 2, 3)).reshape(head_shape)

    cumulative, last_cum, decay_mask = decay_tables(log_decay)
    rise_rows = to_rows(jnp.exp(cumulative))
    fall_rows = to_rows(jnp.exp(last_cum - cumulative))
    scaled_query = (rise_rows * q_split).astype(jnp.bfloat16)
    scaled_key = (fall_rows * k_split).astype(jnp.bfloat16)
    update = jnp.einsum("bjhd,bjhe->bhde", scaled_key, v_split, preferred_element_type=jnp.float32)

    local_grad = jnp.einsum(
        "bihd,bihe->bhde", scaled_query, g_split, preferred_element_type=jnp.float32
    )
    group_count = lax.axis_size("zg")
    inner_count = lax.axis_size("zl")
    core = lax.axis_index("core")
    second = core == 1
    pairs = [(0, 1), (1, 0)]
    last = last_cum[..., 0]
    other_update, other_grad, other_last = lax.ppermute((update, local_grad, last), "core", pairs)

    def order(mine, other):
        return jnp.where(second, other, mine), jnp.where(second, mine, other)

    update_lo, update_hi = order(update, other_update)
    grad_lo, grad_hi = order(local_grad, other_grad)
    last_lo, last_hi = order(last, other_last)
    keep_lo = jnp.exp(last_lo)[..., None, None]
    keep_hi = jnp.exp(last_hi)[..., None, None]
    chip_update = keep_hi * update_lo + update_hi
    chip_grad = keep_lo * grad_hi + grad_lo
    half = width // 2
    band = half // inner_count

    def my_half(state):
        return lax.dynamic_slice_in_dim(state, core * half, half, axis=2)

    chip_last = jnp.broadcast_to((last_lo + last_hi)[..., None], (batch_count, head_count, width))
    last_piece = jnp.broadcast_to(
        chip_last[None, :, :, None, :], (inner_count, batch_count, head_count, 1, width)
    )
    send = jnp.concatenate(
        [to_pieces(my_half(chip_update), inner_count), to_pieces(my_half(chip_grad), inner_count), last_piece],
        axis=3,
    )
    got = lax.all_to_all(send, "zl", 0, 0, tiled=True)
    chip_states = got[:, :, :, :band]
    chip_grads = got[:, :, :, band : 2 * band]
    chip_lasts = got[:, :, :, 2 * band, 0]
    forward_w, backward_w = block_weights(chip_lasts)
    within_state = mix_blocks(forward_w, chip_states)
    within_grad = mix_blocks(backward_w, chip_grads)
    inclusive = jnp.cumsum(chip_lasts, axis=0)
    exclusive = inclusive - chip_lasts
    total = inclusive[-1]
    after_rise = jnp.exp(total[None] - inclusive)[..., None, None]
    before_rise = jnp.exp(exclusive)[..., None, None]
    group_state = jnp.sum(after_rise * chip_states, axis=0)
    group_grad = jnp.sum(before_rise * chip_grads, axis=0)
    group_last = jnp.broadcast_to(total[..., None], (batch_count, head_count, width))
    group_last = jnp.broadcast_to(
        group_last[None, :, :, None, :], (group_count, batch_count, head_count, 1, width)
    )
    cut = band // group_count
    send_groups = jnp.concatenate(
        [to_pieces(group_state, group_count), to_pieces(group_grad, group_count), group_last], axis=3
    )
    got_groups = lax.all_to_all(send_groups, "zg", 0, 0, tiled=True)
    forward_g, backward_g = block_weights(got_groups[:, :, :, 2 * cut, 0])
    mixed_groups = jnp.stack(
        [
            mix_blocks(forward_g, got_groups[:, :, :, :cut]),
            mix_blocks(backward_g, got_groups[:, :, :, cut : 2 * cut]),
        ],
        axis=1,
    )
    back_groups = lax.all_to_all(mixed_groups, "zg", 0, 0, tiled=True)
    entering_group = from_pieces(back_groups[:, 0])
    leaving_group = from_pieces(back_groups[:, 1])
    state_pieces = within_state + before_rise * entering_group[None]
    grad_pieces = within_grad + after_rise * leaving_group[None]
    mixed = jnp.stack([state_pieces, grad_pieces], axis=1)
    back = lax.all_to_all(mixed, "zl", 0, 0, tiled=True)
    halves = jnp.stack([from_pieces(back[:, 0]), from_pieces(back[:, 1])])
    other_halves = lax.ppermute(halves, "core", pairs)
    low_rows, high_rows = order(halves, other_halves)
    entering = jnp.concatenate([low_rows, high_rows], axis=3)
    state_b = jnp.where(second, keep_lo * entering[0] + update_lo, entering[0]).astype(jnp.bfloat16)
    carried_b = jnp.where(second, entering[1], keep_hi * entering[1] + grad_hi).astype(jnp.bfloat16)

    scores = jnp.einsum("bihd,bjhd->bhij", q_split, k_split, preferred_element_type=jnp.float32)
    attn_weights = (scores * decay_mask).astype(jnp.bfloat16)
    grad_raw = jnp.einsum("bihe,bjhe->bhij", g_split, v_split, preferred_element_type=jnp.float32)
    grad_scores = (grad_raw * decay_mask).astype(jnp.bfloat16)
    attended = jnp.einsum(
        "bhij,bjhd->bihd", attn_weights, v_split, preferred_element_type=jnp.float32
    )
    attended = attended + jnp.einsum(
        "bihd,bhde->bihe", scaled_query, state_b, preferred_element_type=jnp.float32
    )
    query_part = jnp.einsum(
        "bhij,bjhd->bihd", grad_scores, k_split, preferred_element_type=jnp.float32
    )
    query_part = query_part + rise_rows * jnp.einsum(
        "bihe,bhde->bihd", g_split, state_b, preferred_element_type=jnp.float32
    )
    key_part = jnp.einsum(
        "bhij,bihd->bjhd", grad_scores, q_split, preferred_element_type=jnp.float32
    )
    key_part = key_part + fall_rows * jnp.einsum(
        "bjhe,bhde->bjhd", v_split, carried_b, preferred_element_type=jnp.float32
    )
    value_part = jnp.einsum(
        "bhij,bihe->bjhe", attn_weights, g_split, preferred_element_type=jnp.float32
    )
    value_part = value_part + fall_rows * jnp.einsum(
        "bjhd,bhde->bjhe", k_split, carried_b, preferred_element_type=jnp.float32
    )

    outs = jnp.stack([attended, query_part, key_part, value_part]).astype(jnp.bfloat16)
    outs = outs.reshape(4, batch_count, uly_count, positions // uly_count, width_heads)
    outs = jnp.transpose(outs, (2, 0, 1, 3, 4))
    outs = lax.all_to_all(outs, "uly", 0, 0, tiled=True)
    outs = jnp.transpose(outs, (1, 2, 3, 0, 4)).reshape(
        4, batch_count, positions // uly_count, uly_count * width_heads
    )
    return (outs[0], outs[1], outs[2], outs[3])


def solution(mesh):
    ctx_count, uly_count = mesh.shape["ctx"], mesh.shape["uly"]
    inner = 4 if ctx_count % 8 == 0 else 1
    grid = mesh.devices.reshape(ctx_count // (2 * inner), inner, 2, uly_count)
    chips = Mesh(grid, ("zg", "zl", "core", "uly"))
    placed = (
        P(None, ("zg", "zl", "core"), "uly"),
        P(None, ("zg", "zl", "core"), "uly"),
        P(None, ("zg", "zl", "core"), "uly"),
        P(None, ("zg", "zl", "core", "uly"), None),
        P(None, "uly", ("zg", "zl", "core")),
    )
    return jax.shard_map(
        local,
        mesh=chips,
        in_specs=placed,
        out_specs=(
            P(None, ("zg", "zl", "core", "uly"), None),
            P(None, ("zg", "zl", "core", "uly"), None),
            P(None, ("zg", "zl", "core", "uly"), None),
            P(None, ("zg", "zl", "core", "uly"), None),
        ),
        check_vma=False,
    )
```

```python
import jax
import jax.numpy as jnp
from jax import lax
from jax.sharding import Mesh, PartitionSpec as P


def decay_tables(log_decay):
    cumulative = jnp.cumsum(log_decay, axis=-1)
    last_cum = cumulative[..., -1:]
    block_len = log_decay.shape[-1]
    row_ids = lax.broadcasted_iota(jnp.int32, (block_len, block_len), 0)
    col_ids = lax.broadcasted_iota(jnp.int32, (block_len, block_len), 1)
    lower_tri = row_ids >= col_ids
    spread = cumulative[..., :, None] - cumulative[..., None, :]
    decay_mask = jnp.where(lower_tri, jnp.exp(jnp.where(lower_tri, spread, 0.0)), 0.0)
    return (cumulative, last_cum, decay_mask)


def to_rows(table):
    return jnp.swapaxes(table, 1, 2)[..., None]


def to_pieces(state, count):
    batch_count, head_count, rows, width = state.shape
    banded = state.reshape(batch_count, head_count, count, rows // count, width)
    return jnp.transpose(banded, (2, 0, 1, 3, 4))


def from_pieces(pieces):
    count, batch_count, head_count, rows, width = pieces.shape
    return jnp.transpose(pieces, (1, 2, 0, 3, 4)).reshape(batch_count, head_count, count * rows, width)


def block_weights(last_all):
    count = last_all.shape[0]
    inclusive = jnp.cumsum(last_all, axis=0)
    exclusive = inclusive - last_all
    inc = jnp.transpose(inclusive, (1, 2, 0))
    exc = jnp.transpose(exclusive, (1, 2, 0))
    row_ids = lax.broadcasted_iota(jnp.int32, (count, count), 0)
    col_ids = lax.broadcasted_iota(jnp.int32, (count, count), 1)
    earlier = col_ids < row_ids
    later = col_ids > row_ids
    forward_gap = exc[..., :, None] - inc[..., None, :]
    backward_gap = exc[..., None, :] - inc[..., :, None]
    forward = jnp.where(earlier, jnp.exp(jnp.where(earlier, forward_gap, 0.0)), 0.0)
    backward = jnp.where(later, jnp.exp(jnp.where(later, backward_gap, 0.0)), 0.0)
    return forward, backward


def mix_blocks(weights, pieces):
    return jnp.einsum(
        "bhcd,dbhrx->cbhrx", weights, pieces, precision=lax.Precision.HIGHEST,
        preferred_element_type=jnp.float32,
    )


def local(query_heads, key_heads, value_heads, grad_out, log_decay):
    batch_count, positions, width_heads = query_heads.shape
    head_count = log_decay.shape[1]
    width = width_heads // head_count
    uly_count = lax.axis_size("uly")
    head_shape = (batch_count, positions, head_count, width)
    q_split = query_heads.reshape(head_shape)
    k_split = key_heads.reshape(head_shape)
    v_split = value_heads.reshape(head_shape)

    rows_in = grad_out.shape[1]
    g_parts = grad_out.reshape(batch_count, rows_in, uly_count, width_heads)
    g_parts = jnp.transpose(g_parts, (2, 0, 1, 3))
    g_parts = lax.all_to_all(g_parts, "uly", 0, 0, tiled=True)
    g_split = jnp.transpose(g_parts, (1, 0, 2, 3)).reshape(head_shape)

    cumulative, last_cum, decay_mask = decay_tables(log_decay)
    rise_rows = to_rows(jnp.exp(cumulative))
    fall_rows = to_rows(jnp.exp(last_cum - cumulative))
    scaled_query = (rise_rows * q_split).astype(jnp.bfloat16)
    scaled_key = (fall_rows * k_split).astype(jnp.bfloat16)
    update = jnp.einsum("bjhd,bjhe->bhde", scaled_key, v_split, preferred_element_type=jnp.float32)

    local_grad = jnp.einsum(
        "bihd,bihe->bhde", scaled_query, g_split, preferred_element_type=jnp.float32
    )
    group_count = lax.axis_size("zg")
    inner_count = lax.axis_size("zl")
    core = lax.axis_index("core")
    second = core == 1
    pairs = [(0, 1), (1, 0)]
    last = last_cum[..., 0]
    other_update, other_grad, other_last = lax.ppermute((update, local_grad, last), "core", pairs)

    def order(mine, other):
        return jnp.where(second, other, mine), jnp.where(second, mine, other)

    update_lo, update_hi = order(update, other_update)
    grad_lo, grad_hi = order(local_grad, other_grad)
    last_lo, last_hi = order(last, other_last)
    keep_lo = jnp.exp(last_lo)[..., None, None]
    keep_hi = jnp.exp(last_hi)[..., None, None]
    chip_update = keep_hi * update_lo + update_hi
    chip_grad = keep_lo * grad_hi + grad_lo
    half = width // 2
    band = half // inner_count

    def my_half(state):
        return lax.dynamic_slice_in_dim(state, core * half, half, axis=2)

    chip_last = jnp.broadcast_to((last_lo + last_hi)[..., None], (batch_count, head_count, width))
    last_piece = jnp.broadcast_to(
        chip_last[None, :, :, None, :], (inner_count, batch_count, head_count, 1, width)
    )
    send = jnp.concatenate(
        [to_pieces(my_half(chip_update), inner_count), to_pieces(my_half(chip_grad), inner_count), last_piece],
        axis=3,
    )
    got = lax.all_to_all(send, "zl", 0, 0, tiled=True)
    chip_states = got[:, :, :, :band]
    chip_grads = got[:, :, :, band : 2 * band]
    chip_lasts = got[:, :, :, 2 * band, 0]
    forward_w, backward_w = block_weights(chip_lasts)
    within_state = mix_blocks(forward_w, chip_states)
    within_grad = mix_blocks(backward_w, chip_grads)
    inclusive = jnp.cumsum(chip_lasts, axis=0)
    exclusive = inclusive - chip_lasts
    total = inclusive[-1]
    after_rise = jnp.exp(total[None] - inclusive)[..., None, None]
    before_rise = jnp.exp(exclusive)[..., None, None]
    group_state = jnp.sum(after_rise * chip_states, axis=0)
    group_grad = jnp.sum(before_rise * chip_grads, axis=0)
    group_keep = jnp.exp(total)[..., None, None]
    upward = [(index, index + 1) for index in range(group_count - 1)]
    downward = [(index + 1, index) for index in range(group_count - 1)]
    entering_group = jnp.zeros_like(group_state)
    leaving_group = jnp.zeros_like(group_grad)
    for _ in range(group_count - 1):
        entering_group, leaving_group = (
            lax.ppermute(group_keep * entering_group + group_state, "zg", upward),
            lax.ppermute(group_keep * leaving_group + group_grad, "zg", downward),
        )
    state_pieces = within_state + before_rise * entering_group[None]
    grad_pieces = within_grad + after_rise * leaving_group[None]
    mixed = jnp.stack([state_pieces, grad_pieces], axis=1)
    back = lax.all_to_all(mixed, "zl", 0, 0, tiled=True)
    halves = jnp.stack([from_pieces(back[:, 0]), from_pieces(back[:, 1])])
    other_halves = lax.ppermute(halves, "core", pairs)
    low_rows, high_rows = order(halves, other_halves)
    entering = jnp.concatenate([low_rows, high_rows], axis=3)
    state_b = jnp.where(second, keep_lo * entering[0] + update_lo, entering[0]).astype(jnp.bfloat16)
    carried_b = jnp.where(second, entering[1], keep_hi * entering[1] + grad_hi).astype(jnp.bfloat16)

    scores = jnp.einsum("bihd,bjhd->bhij", q_split, k_split, preferred_element_type=jnp.float32)
    attn_weights = (scores * decay_mask).astype(jnp.bfloat16)
    grad_raw = jnp.einsum("bihe,bjhe->bhij", g_split, v_split, preferred_element_type=jnp.float32)
    grad_scores = (grad_raw * decay_mask).astype(jnp.bfloat16)
    attended = jnp.einsum(
        "bhij,bjhd->bihd", attn_weights, v_split, preferred_element_type=jnp.float32
    )
    attended = attended + jnp.einsum(
        "bihd,bhde->bihe", scaled_query, state_b, preferred_element_type=jnp.float32
    )
    query_part = jnp.einsum(
        "bhij,bjhd->bihd", grad_scores, k_split, preferred_element_type=jnp.float32
    )
    query_part = query_part + rise_rows * jnp.einsum(
        "bihe,bhde->bihd", g_split, state_b, preferred_element_type=jnp.float32
    )
    key_part = jnp.einsum(
        "bhij,bihd->bjhd", grad_scores, q_split, preferred_element_type=jnp.float32
    )
    key_part = key_part + fall_rows * jnp.einsum(
        "bjhe,bhde->bjhd", v_split, carried_b, preferred_element_type=jnp.float32
    )
    value_part = jnp.einsum(
        "bhij,bihe->bjhe", attn_weights, g_split, preferred_element_type=jnp.float32
    )
    value_part = value_part + fall_rows * jnp.einsum(
        "bjhd,bhde->bjhe", k_split, carried_b, preferred_element_type=jnp.float32
    )

    outs = jnp.stack([attended, query_part, key_part, value_part]).astype(jnp.bfloat16)
    outs = outs.reshape(4, batch_count, uly_count, positions // uly_count, width_heads)
    outs = jnp.transpose(outs, (2, 0, 1, 3, 4))
    outs = lax.all_to_all(outs, "uly", 0, 0, tiled=True)
    outs = jnp.transpose(outs, (1, 2, 3, 0, 4)).reshape(
        4, batch_count, positions // uly_count, uly_count * width_heads
    )
    return (outs[0], outs[1], outs[2], outs[3])


def solution(mesh):
    ctx_count, uly_count = mesh.shape["ctx"], mesh.shape["uly"]
    inner = 8 if ctx_count % 16 == 0 else 1
    grid = mesh.devices.reshape(ctx_count // (2 * inner), inner, 2, uly_count)
    chips = Mesh(grid, ("zg", "zl", "core", "uly"))
    placed = (
        P(None, ("zg", "zl", "core"), "uly"),
        P(None, ("zg", "zl", "core"), "uly"),
        P(None, ("zg", "zl", "core"), "uly"),
        P(None, ("zg", "zl", "core", "uly"), None),
        P(None, "uly", ("zg", "zl", "core")),
    )
    return jax.shard_map(
        local,
        mesh=chips,
        in_specs=placed,
        out_specs=(
            P(None, ("zg", "zl", "core", "uly"), None),
            P(None, ("zg", "zl", "core", "uly"), None),
            P(None, ("zg", "zl", "core", "uly"), None),
            P(None, ("zg", "zl", "core", "uly"), None),
        ),
        check_vma=False,
    )
```

```python
import jax
import jax.numpy as jnp
from jax import lax
from jax.sharding import Mesh, PartitionSpec as P


def decay_tables(log_decay):
    cumulative = jnp.cumsum(log_decay, axis=-1)
    last_cum = cumulative[..., -1:]
    block_len = log_decay.shape[-1]
    row_ids = lax.broadcasted_iota(jnp.int32, (block_len, block_len), 0)
    col_ids = lax.broadcasted_iota(jnp.int32, (block_len, block_len), 1)
    lower_tri = row_ids >= col_ids
    spread = cumulative[..., :, None] - cumulative[..., None, :]
    decay_mask = jnp.where(lower_tri, jnp.exp(jnp.where(lower_tri, spread, 0.0)), 0.0)
    return (cumulative, last_cum, decay_mask)


def to_rows(table):
    return jnp.swapaxes(table, 1, 2)[..., None]


def to_pieces(state, count):
    batch_count, head_count, rows, width = state.shape
    banded = state.reshape(batch_count, head_count, count, rows // count, width)
    return jnp.transpose(banded, (2, 0, 1, 3, 4))


def from_pieces(pieces):
    count, batch_count, head_count, rows, width = pieces.shape
    return jnp.transpose(pieces, (1, 2, 0, 3, 4)).reshape(batch_count, head_count, count * rows, width)


def block_weights(last_all):
    count = last_all.shape[0]
    inclusive = jnp.cumsum(last_all, axis=0)
    exclusive = inclusive - last_all
    inc = jnp.transpose(inclusive, (1, 2, 0))
    exc = jnp.transpose(exclusive, (1, 2, 0))
    row_ids = lax.broadcasted_iota(jnp.int32, (count, count), 0)
    col_ids = lax.broadcasted_iota(jnp.int32, (count, count), 1)
    earlier = col_ids < row_ids
    later = col_ids > row_ids
    forward_gap = exc[..., :, None] - inc[..., None, :]
    backward_gap = exc[..., None, :] - inc[..., :, None]
    forward = jnp.where(earlier, jnp.exp(jnp.where(earlier, forward_gap, 0.0)), 0.0)
    backward = jnp.where(later, jnp.exp(jnp.where(later, backward_gap, 0.0)), 0.0)
    return forward, backward


def mix_blocks(weights, pieces):
    return jnp.einsum(
        "bhcd,dbhrx->cbhrx", weights, pieces, precision=lax.Precision.HIGHEST,
        preferred_element_type=jnp.float32,
    )


def local(query_heads, key_heads, value_heads, grad_out, log_decay):
    batch_count, positions, width_heads = query_heads.shape
    head_count = log_decay.shape[1]
    width = width_heads // head_count
    uly_count = lax.axis_size("uly")
    head_shape = (batch_count, positions, head_count, width)
    q_split = query_heads.reshape(head_shape)
    k_split = key_heads.reshape(head_shape)
    v_split = value_heads.reshape(head_shape)

    rows_in = grad_out.shape[1]
    g_parts = grad_out.reshape(batch_count, rows_in, uly_count, width_heads)
    g_parts = jnp.transpose(g_parts, (2, 0, 1, 3))
    g_parts = lax.all_to_all(g_parts, "uly", 0, 0, tiled=True)
    g_split = jnp.transpose(g_parts, (1, 0, 2, 3)).reshape(head_shape)

    cumulative, last_cum, decay_mask = decay_tables(log_decay)
    rise_rows = to_rows(jnp.exp(cumulative))
    fall_rows = to_rows(jnp.exp(last_cum - cumulative))
    scaled_query = (rise_rows * q_split).astype(jnp.bfloat16)
    scaled_key = (fall_rows * k_split).astype(jnp.bfloat16)
    update = jnp.einsum("bjhd,bjhe->bhde", scaled_key, v_split, preferred_element_type=jnp.float32)

    local_grad = jnp.einsum(
        "bihd,bihe->bhde", scaled_query, g_split, preferred_element_type=jnp.float32
    )
    chip_count = lax.axis_size("z")
    core = lax.axis_index("core")
    second = core == 1
    pairs = [(0, 1), (1, 0)]
    last = last_cum[..., 0]
    other_update, other_grad, other_last = lax.ppermute((update, local_grad, last), "core", pairs)

    def order(mine, other):
        return jnp.where(second, other, mine), jnp.where(second, mine, other)

    update_lo, update_hi = order(update, other_update)
    grad_lo, grad_hi = order(local_grad, other_grad)
    last_lo, last_hi = order(last, other_last)
    keep_lo = jnp.exp(last_lo)[..., None, None]
    keep_hi = jnp.exp(last_hi)[..., None, None]
    chip_update = keep_hi * update_lo + update_hi
    chip_grad = keep_lo * grad_hi + grad_lo
    half = width // 2

    def my_half(state):
        return lax.dynamic_slice_in_dim(state, core * half, half, axis=2)

    chip_index = lax.axis_index("z")
    chip_ids = lax.broadcasted_iota(jnp.int32, (chip_count, 1, 1), 0)
    chip_last = jnp.broadcast_to((last_lo + last_hi)[..., None, None], (batch_count, head_count, 1, width))
    states_all = lax.all_gather(jnp.concatenate([my_half(chip_update), chip_last], axis=2), "z")
    lasts_all = states_all[:, :, :, half, 0]
    inclusive = jnp.cumsum(lasts_all, axis=0)
    exclusive = inclusive - lasts_all
    earlier = chip_ids < chip_index
    forward_gap = jnp.where(earlier, exclusive[chip_index][None] - inclusive, 0.0)
    forward_w = jnp.where(earlier, jnp.exp(forward_gap), 0.0)[..., None, None]
    state_half = jnp.sum(forward_w * states_all[:, :, :, :half], axis=0)
    grads_all = lax.all_gather(my_half(chip_grad), "z")
    later = chip_ids > chip_index
    backward_gap = jnp.where(later, exclusive - inclusive[chip_index][None], 0.0)
    backward_w = jnp.where(later, jnp.exp(backward_gap), 0.0)[..., None, None]
    grad_half = jnp.sum(backward_w * grads_all, axis=0)
    halves = jnp.stack([state_half, grad_half])
    other_halves = lax.ppermute(halves, "core", pairs)
    low_rows, high_rows = order(halves, other_halves)
    entering = jnp.concatenate([low_rows, high_rows], axis=3)
    state_b = jnp.where(second, keep_lo * entering[0] + update_lo, entering[0]).astype(jnp.bfloat16)
    carried_b = jnp.where(second, entering[1], keep_hi * entering[1] + grad_hi).astype(jnp.bfloat16)

    scores = jnp.einsum("bihd,bjhd->bhij", q_split, k_split, preferred_element_type=jnp.float32)
    attn_weights = (scores * decay_mask).astype(jnp.bfloat16)
    grad_raw = jnp.einsum("bihe,bjhe->bhij", g_split, v_split, preferred_element_type=jnp.float32)
    grad_scores = (grad_raw * decay_mask).astype(jnp.bfloat16)
    attended = jnp.einsum(
        "bhij,bjhd->bihd", attn_weights, v_split, preferred_element_type=jnp.float32
    )
    attended = attended + jnp.einsum(
        "bihd,bhde->bihe", scaled_query, state_b, preferred_element_type=jnp.float32
    )
    query_part = jnp.einsum(
        "bhij,bjhd->bihd", grad_scores, k_split, preferred_element_type=jnp.float32
    )
    query_part = query_part + rise_rows * jnp.einsum(
        "bihe,bhde->bihd", g_split, state_b, preferred_element_type=jnp.float32
    )
    key_part = jnp.einsum(
        "bhij,bihd->bjhd", grad_scores, q_split, preferred_element_type=jnp.float32
    )
    key_part = key_part + fall_rows * jnp.einsum(
        "bjhe,bhde->bjhd", v_split, carried_b, preferred_element_type=jnp.float32
    )
    value_part = jnp.einsum(
        "bhij,bihe->bjhe", attn_weights, g_split, preferred_element_type=jnp.float32
    )
    value_part = value_part + fall_rows * jnp.einsum(
        "bjhd,bhde->bjhe", k_split, carried_b, preferred_element_type=jnp.float32
    )

    outs = jnp.stack([attended, query_part, key_part, value_part]).astype(jnp.bfloat16)
    outs = outs.reshape(4, batch_count, uly_count, positions // uly_count, width_heads)
    outs = jnp.transpose(outs, (2, 0, 1, 3, 4))
    outs = lax.all_to_all(outs, "uly", 0, 0, tiled=True)
    outs = jnp.transpose(outs, (1, 2, 3, 0, 4)).reshape(
        4, batch_count, positions // uly_count, uly_count * width_heads
    )
    return (outs[0], outs[1], outs[2], outs[3])


def solution(mesh):
    ctx_count, uly_count = mesh.shape["ctx"], mesh.shape["uly"]
    grid = mesh.devices.reshape(ctx_count // 2, 2, uly_count)
    chips = Mesh(grid, ("z", "core", "uly"))
    placed = (
        P(None, ("z", "core"), "uly"),
        P(None, ("z", "core"), "uly"),
        P(None, ("z", "core"), "uly"),
        P(None, ("z", "core", "uly"), None),
        P(None, "uly", ("z", "core")),
    )
    return jax.shard_map(
        local,
        mesh=chips,
        in_specs=placed,
        out_specs=(
            P(None, ("z", "core", "uly"), None),
            P(None, ("z", "core", "uly"), None),
            P(None, ("z", "core", "uly"), None),
            P(None, ("z", "core", "uly"), None),
        ),
        check_vma=False,
    )
```

```python
import jax
import jax.numpy as jnp
from jax import lax
from jax.sharding import Mesh, PartitionSpec as P


def decay_tables(log_decay):
    cumulative = jnp.cumsum(log_decay, axis=-1)
    last_cum = cumulative[..., -1:]
    block_len = log_decay.shape[-1]
    row_ids = lax.broadcasted_iota(jnp.int32, (block_len, block_len), 0)
    col_ids = lax.broadcasted_iota(jnp.int32, (block_len, block_len), 1)
    lower_tri = row_ids >= col_ids
    spread = cumulative[..., :, None] - cumulative[..., None, :]
    decay_mask = jnp.where(lower_tri, jnp.exp(jnp.where(lower_tri, spread, 0.0)), 0.0)
    return (cumulative, last_cum, decay_mask)


def to_rows(table):
    return jnp.swapaxes(table, 1, 2)[..., None]


def to_pieces(state, count):
    batch_count, head_count, rows, width = state.shape
    banded = state.reshape(batch_count, head_count, count, rows // count, width)
    return jnp.transpose(banded, (2, 0, 1, 3, 4))


def from_pieces(pieces):
    count, batch_count, head_count, rows, width = pieces.shape
    return jnp.transpose(pieces, (1, 2, 0, 3, 4)).reshape(batch_count, head_count, count * rows, width)


def block_weights(last_all):
    count = last_all.shape[0]
    inclusive = jnp.cumsum(last_all, axis=0)
    exclusive = inclusive - last_all
    inc = jnp.transpose(inclusive, (1, 2, 0))
    exc = jnp.transpose(exclusive, (1, 2, 0))
    row_ids = lax.broadcasted_iota(jnp.int32, (count, count), 0)
    col_ids = lax.broadcasted_iota(jnp.int32, (count, count), 1)
    earlier = col_ids < row_ids
    later = col_ids > row_ids
    forward_gap = exc[..., :, None] - inc[..., None, :]
    backward_gap = exc[..., None, :] - inc[..., :, None]
    forward = jnp.where(earlier, jnp.exp(jnp.where(earlier, forward_gap, 0.0)), 0.0)
    backward = jnp.where(later, jnp.exp(jnp.where(later, backward_gap, 0.0)), 0.0)
    return forward, backward


def mix_blocks(weights, pieces):
    return jnp.einsum(
        "bhcd,dbhrx->cbhrx", weights, pieces, precision=lax.Precision.HIGHEST,
        preferred_element_type=jnp.float32,
    )


def local(query_heads, key_heads, value_heads, grad_out, log_decay):
    batch_count, positions, width_heads = query_heads.shape
    head_count = log_decay.shape[1]
    width = width_heads // head_count
    uly_count = lax.axis_size("uly")
    head_shape = (batch_count, positions, head_count, width)
    q_split = query_heads.reshape(head_shape)
    k_split = key_heads.reshape(head_shape)
    v_split = value_heads.reshape(head_shape)

    rows_in = grad_out.shape[1]
    g_parts = grad_out.reshape(batch_count, rows_in, uly_count, width_heads)
    g_parts = jnp.transpose(g_parts, (2, 0, 1, 3))
    g_parts = lax.all_to_all(g_parts, "uly", 0, 0, tiled=True)
    g_split = jnp.transpose(g_parts, (1, 0, 2, 3)).reshape(head_shape)

    cumulative, last_cum, decay_mask = decay_tables(log_decay)
    rise_rows = to_rows(jnp.exp(cumulative))
    fall_rows = to_rows(jnp.exp(last_cum - cumulative))
    scaled_query = (rise_rows * q_split).astype(jnp.bfloat16)
    scaled_key = (fall_rows * k_split).astype(jnp.bfloat16)
    update = jnp.einsum("bjhd,bjhe->bhde", scaled_key, v_split, preferred_element_type=jnp.float32)

    local_grad = jnp.einsum(
        "bihd,bihe->bhde", scaled_query, g_split, preferred_element_type=jnp.float32
    )
    chip_count = lax.axis_size("z")
    core = lax.axis_index("core")
    second = core == 1
    pairs = [(0, 1), (1, 0)]
    last = last_cum[..., 0]
    last_row = jnp.broadcast_to(last[..., None, None], (batch_count, head_count, 1, width))
    other_packed = lax.ppermute(jnp.concatenate([update, last_row], axis=2), "core", pairs)
    other_update = other_packed[:, :, :width]
    other_last = other_packed[:, :, width, 0]
    other_grad = lax.ppermute(local_grad, "core", pairs)

    def order(mine, other):
        return jnp.where(second, other, mine), jnp.where(second, mine, other)

    update_lo, update_hi = order(update, other_update)
    grad_lo, grad_hi = order(local_grad, other_grad)
    last_lo, last_hi = order(last, other_last)
    keep_lo = jnp.exp(last_lo)[..., None, None]
    keep_hi = jnp.exp(last_hi)[..., None, None]
    chip_update = keep_hi * update_lo + update_hi
    chip_grad = keep_lo * grad_hi + grad_lo
    half = width // 2
    band = half // chip_count

    def my_half(state):
        return lax.dynamic_slice_in_dim(state, core * half, half, axis=2)

    chip_last = jnp.broadcast_to((last_lo + last_hi)[..., None], (batch_count, head_count, width))
    last_piece = jnp.broadcast_to(
        chip_last[None, :, :, None, :], (chip_count, batch_count, head_count, 1, width)
    )
    send = jnp.concatenate(
        [to_pieces(my_half(chip_update), chip_count), to_pieces(my_half(chip_grad), chip_count), last_piece],
        axis=3,
    )
    got = lax.all_to_all(send, "z", 0, 0, tiled=True)
    forward_w, backward_w = block_weights(got[:, :, :, 2 * band, 0])
    mixed = jnp.stack(
        [
            mix_blocks(forward_w, got[:, :, :, :band]),
            mix_blocks(backward_w, got[:, :, :, band : 2 * band]),
        ],
        axis=1,
    )
    back = lax.all_to_all(mixed, "z", 0, 0, tiled=True)
    halves = jnp.stack([from_pieces(back[:, 0]), from_pieces(back[:, 1])])
    other_halves = lax.ppermute(halves, "core", pairs)
    low_rows, high_rows = order(halves, other_halves)
    entering = jnp.concatenate([low_rows, high_rows], axis=3)
    state_b = jnp.where(second, keep_lo * entering[0] + update_lo, entering[0]).astype(jnp.bfloat16)
    carried_b = jnp.where(second, entering[1], keep_hi * entering[1] + grad_hi).astype(jnp.bfloat16)

    scores = jnp.einsum("bihd,bjhd->bhij", q_split, k_split, preferred_element_type=jnp.float32)
    attn_weights = (scores * decay_mask).astype(jnp.bfloat16)
    grad_raw = jnp.einsum("bihe,bjhe->bhij", g_split, v_split, preferred_element_type=jnp.float32)
    grad_scores = (grad_raw * decay_mask).astype(jnp.bfloat16)
    attended = jnp.einsum(
        "bhij,bjhd->bihd", attn_weights, v_split, preferred_element_type=jnp.float32
    )
    attended = attended + jnp.einsum(
        "bihd,bhde->bihe", scaled_query, state_b, preferred_element_type=jnp.float32
    )
    query_part = jnp.einsum(
        "bhij,bjhd->bihd", grad_scores, k_split, preferred_element_type=jnp.float32
    )
    query_part = query_part + rise_rows * jnp.einsum(
        "bihe,bhde->bihd", g_split, state_b, preferred_element_type=jnp.float32
    )
    key_part = jnp.einsum(
        "bhij,bihd->bjhd", grad_scores, q_split, preferred_element_type=jnp.float32
    )
    key_part = key_part + fall_rows * jnp.einsum(
        "bjhe,bhde->bjhd", v_split, carried_b, preferred_element_type=jnp.float32
    )
    value_part = jnp.einsum(
        "bhij,bihe->bjhe", attn_weights, g_split, preferred_element_type=jnp.float32
    )
    value_part = value_part + fall_rows * jnp.einsum(
        "bjhd,bhde->bjhe", k_split, carried_b, preferred_element_type=jnp.float32
    )

    outs = jnp.stack([attended, query_part, key_part, value_part]).astype(jnp.bfloat16)
    outs = outs.reshape(4, batch_count, uly_count, positions // uly_count, width_heads)
    outs = jnp.transpose(outs, (2, 0, 1, 3, 4))
    outs = lax.all_to_all(outs, "uly", 0, 0, tiled=True)

    def to_tokens(index):
        return jnp.transpose(outs[:, index], (1, 2, 0, 3)).reshape(
            batch_count, positions // uly_count, uly_count * width_heads
        )

    return (to_tokens(0), to_tokens(1), to_tokens(2), to_tokens(3))


def solution(mesh):
    ctx_count, uly_count = mesh.shape["ctx"], mesh.shape["uly"]
    grid = mesh.devices.reshape(ctx_count // 2, 2, uly_count)
    chips = Mesh(grid, ("z", "core", "uly"))
    placed = (
        P(None, ("z", "core"), "uly"),
        P(None, ("z", "core"), "uly"),
        P(None, ("z", "core"), "uly"),
        P(None, ("z", "core", "uly"), None),
        P(None, "uly", ("z", "core")),
    )
    return jax.shard_map(
        local,
        mesh=chips,
        in_specs=placed,
        out_specs=(
            P(None, ("z", "core", "uly"), None),
            P(None, ("z", "core", "uly"), None),
            P(None, ("z", "core", "uly"), None),
            P(None, ("z", "core", "uly"), None),
        ),
        check_vma=False,
    )
```

```python
import jax
import jax.numpy as jnp
from jax import lax
from jax.sharding import Mesh, PartitionSpec as P


def decay_tables(log_decay):
    cumulative = jnp.cumsum(log_decay, axis=-1)
    last_cum = cumulative[..., -1:]
    block_len = log_decay.shape[-1]
    row_ids = lax.broadcasted_iota(jnp.int32, (block_len, block_len), 0)
    col_ids = lax.broadcasted_iota(jnp.int32, (block_len, block_len), 1)
    lower_tri = row_ids >= col_ids
    spread = cumulative[..., :, None] - cumulative[..., None, :]
    decay_mask = jnp.where(lower_tri, jnp.exp(jnp.where(lower_tri, spread, 0.0)), 0.0)
    return (cumulative, last_cum, decay_mask)


def to_rows(table):
    return jnp.swapaxes(table, 1, 2)[..., None]


def to_pieces(state, count):
    batch_count, head_count, rows, width = state.shape
    banded = state.reshape(batch_count, head_count, count, rows // count, width)
    return jnp.transpose(banded, (2, 0, 1, 3, 4))


def from_pieces(pieces):
    count, batch_count, head_count, rows, width = pieces.shape
    return jnp.transpose(pieces, (1, 2, 0, 3, 4)).reshape(batch_count, head_count, count * rows, width)


def block_weights(last_all):
    count = last_all.shape[0]
    inclusive = jnp.cumsum(last_all, axis=0)
    exclusive = inclusive - last_all
    inc = jnp.transpose(inclusive, (1, 2, 0))
    exc = jnp.transpose(exclusive, (1, 2, 0))
    row_ids = lax.broadcasted_iota(jnp.int32, (count, count), 0)
    col_ids = lax.broadcasted_iota(jnp.int32, (count, count), 1)
    earlier = col_ids < row_ids
    later = col_ids > row_ids
    forward_gap = exc[..., :, None] - inc[..., None, :]
    backward_gap = exc[..., None, :] - inc[..., :, None]
    forward = jnp.where(earlier, jnp.exp(jnp.where(earlier, forward_gap, 0.0)), 0.0)
    backward = jnp.where(later, jnp.exp(jnp.where(later, backward_gap, 0.0)), 0.0)
    return forward, backward


def mix_blocks(weights, pieces):
    return jnp.einsum(
        "bhcd,dbhrx->cbhrx", weights, pieces, precision=lax.Precision.HIGHEST,
        preferred_element_type=jnp.float32,
    )


def local(query_heads, key_heads, value_heads, grad_out, log_decay):
    batch_count, positions, width_heads = query_heads.shape
    head_count = log_decay.shape[1]
    width = width_heads // head_count
    uly_count = lax.axis_size("uly")
    head_shape = (batch_count, positions, head_count, width)
    q_split = query_heads.reshape(head_shape)
    k_split = key_heads.reshape(head_shape)
    v_split = value_heads.reshape(head_shape)

    rows_in = grad_out.shape[1]
    g_parts = grad_out.reshape(batch_count, rows_in, uly_count, width_heads)
    g_parts = jnp.transpose(g_parts, (2, 0, 1, 3))
    g_parts = lax.all_to_all(g_parts, "uly", 0, 0, tiled=True)
    g_split = jnp.transpose(g_parts, (1, 0, 2, 3)).reshape(head_shape)

    cumulative, last_cum, decay_mask = decay_tables(log_decay)
    rise_rows = to_rows(jnp.exp(cumulative))
    fall_rows = to_rows(jnp.exp(last_cum - cumulative))
    scaled_query = (rise_rows * q_split).astype(jnp.bfloat16)
    scaled_key = (fall_rows * k_split).astype(jnp.bfloat16)
    update = jnp.einsum("bjhd,bjhe->bhde", scaled_key, v_split, preferred_element_type=jnp.float32)

    local_grad = jnp.einsum(
        "bihd,bihe->bhde", scaled_query, g_split, preferred_element_type=jnp.float32
    )
    chip_count = lax.axis_size("z")
    core = lax.axis_index("core")
    second = core == 1
    pairs = [(0, 1), (1, 0)]
    last = last_cum[..., 0]
    last_row = jnp.broadcast_to(last[..., None, None], (batch_count, head_count, 1, width))
    other_packed = lax.ppermute(jnp.concatenate([update, last_row], axis=2), "core", pairs)
    other_update = other_packed[:, :, :width]
    other_last = other_packed[:, :, width, 0]
    other_grad = lax.ppermute(local_grad, "core", pairs)

    def order(mine, other):
        return jnp.where(second, other, mine), jnp.where(second, mine, other)

    update_lo, update_hi = order(update, other_update)
    grad_lo, grad_hi = order(local_grad, other_grad)
    last_lo, last_hi = order(last, other_last)
    keep_lo = jnp.exp(last_lo)[..., None, None]
    keep_hi = jnp.exp(last_hi)[..., None, None]
    chip_update = keep_hi * update_lo + update_hi
    chip_grad = keep_lo * grad_hi + grad_lo
    half = width // 2
    band = half // chip_count

    def my_half(state):
        return lax.dynamic_slice_in_dim(state, core * half, half, axis=2)

    chip_last = jnp.broadcast_to((last_lo + last_hi)[..., None], (batch_count, head_count, width))
    last_piece = jnp.broadcast_to(
        chip_last[None, :, :, None, :], (chip_count, batch_count, head_count, 1, width)
    )
    send = jnp.concatenate(
        [to_pieces(my_half(chip_update), chip_count), to_pieces(my_half(chip_grad), chip_count), last_piece],
        axis=3,
    )
    got = lax.all_to_all(send, "z", 0, 0, tiled=True)
    forward_w, backward_w = block_weights(got[:, :, :, 2 * band, 0])
    mixed = jnp.stack(
        [
            mix_blocks(forward_w, got[:, :, :, :band]),
            mix_blocks(backward_w, got[:, :, :, band : 2 * band]),
        ],
        axis=1,
    )
    back = lax.all_to_all(mixed.astype(jnp.bfloat16), "z", 0, 0, tiled=True)
    halves = jnp.stack([from_pieces(back[:, 0]), from_pieces(back[:, 1])])
    other_halves = lax.ppermute(halves, "core", pairs)
    low_rows, high_rows = order(halves, other_halves)
    entering = jnp.concatenate([low_rows, high_rows], axis=3)
    state_b = jnp.where(second, keep_lo * entering[0] + update_lo, entering[0]).astype(jnp.bfloat16)
    carried_b = jnp.where(second, entering[1], keep_hi * entering[1] + grad_hi).astype(jnp.bfloat16)

    scores = jnp.einsum("bihd,bjhd->bhij", q_split, k_split, preferred_element_type=jnp.float32)
    attn_weights = (scores * decay_mask).astype(jnp.bfloat16)
    grad_raw = jnp.einsum("bihe,bjhe->bhij", g_split, v_split, preferred_element_type=jnp.float32)
    grad_scores = (grad_raw * decay_mask).astype(jnp.bfloat16)
    attended = jnp.einsum(
        "bhij,bjhd->bihd", attn_weights, v_split, preferred_element_type=jnp.float32
    )
    attended = attended + jnp.einsum(
        "bihd,bhde->bihe", scaled_query, state_b, preferred_element_type=jnp.float32
    )
    query_part = jnp.einsum(
        "bhij,bjhd->bihd", grad_scores, k_split, preferred_element_type=jnp.float32
    )
    query_part = query_part + rise_rows * jnp.einsum(
        "bihe,bhde->bihd", g_split, state_b, preferred_element_type=jnp.float32
    )
    key_part = jnp.einsum(
        "bhij,bihd->bjhd", grad_scores, q_split, preferred_element_type=jnp.float32
    )
    key_part = key_part + fall_rows * jnp.einsum(
        "bjhe,bhde->bjhd", v_split, carried_b, preferred_element_type=jnp.float32
    )
    value_part = jnp.einsum(
        "bhij,bihe->bjhe", attn_weights, g_split, preferred_element_type=jnp.float32
    )
    value_part = value_part + fall_rows * jnp.einsum(
        "bjhd,bhde->bjhe", k_split, carried_b, preferred_element_type=jnp.float32
    )

    outs = jnp.stack([attended, query_part, key_part, value_part]).astype(jnp.bfloat16)
    outs = outs.reshape(4, batch_count, uly_count, positions // uly_count, width_heads)
    outs = jnp.transpose(outs, (2, 0, 1, 3, 4))
    outs = lax.all_to_all(outs, "uly", 0, 0, tiled=True)

    def to_tokens(index):
        return jnp.transpose(outs[:, index], (1, 2, 0, 3)).reshape(
            batch_count, positions // uly_count, uly_count * width_heads
        )

    return (to_tokens(0), to_tokens(1), to_tokens(2), to_tokens(3))


def solution(mesh):
    ctx_count, uly_count = mesh.shape["ctx"], mesh.shape["uly"]
    grid = mesh.devices.reshape(ctx_count // 2, 2, uly_count)
    chips = Mesh(grid, ("z", "core", "uly"))
    placed = (
        P(None, ("z", "core"), "uly"),
        P(None, ("z", "core"), "uly"),
        P(None, ("z", "core"), "uly"),
        P(None, ("z", "core", "uly"), None),
        P(None, "uly", ("z", "core")),
    )
    return jax.shard_map(
        local,
        mesh=chips,
        in_specs=placed,
        out_specs=(
            P(None, ("z", "core", "uly"), None),
            P(None, ("z", "core", "uly"), None),
            P(None, ("z", "core", "uly"), None),
            P(None, ("z", "core", "uly"), None),
        ),
        check_vma=False,
    )
```

```python
import jax
import jax.numpy as jnp
from jax import lax
from jax.sharding import Mesh, PartitionSpec as P


def decay_tables(log_decay):
    cumulative = jnp.cumsum(log_decay, axis=-1)
    last_cum = cumulative[..., -1:]
    block_len = log_decay.shape[-1]
    row_ids = lax.broadcasted_iota(jnp.int32, (block_len, block_len), 0)
    col_ids = lax.broadcasted_iota(jnp.int32, (block_len, block_len), 1)
    lower_tri = row_ids >= col_ids
    spread = cumulative[..., :, None] - cumulative[..., None, :]
    decay_mask = jnp.where(lower_tri, jnp.exp(jnp.where(lower_tri, spread, 0.0)), 0.0)
    return (cumulative, last_cum, decay_mask)


def to_rows(table):
    return jnp.swapaxes(table, 1, 2)[..., None]


def to_pieces(state, count):
    batch_count, head_count, rows, width = state.shape
    banded = state.reshape(batch_count, head_count, count, rows // count, width)
    return jnp.transpose(banded, (2, 0, 1, 3, 4))


def from_pieces(pieces):
    count, batch_count, head_count, rows, width = pieces.shape
    return jnp.transpose(pieces, (1, 2, 0, 3, 4)).reshape(batch_count, head_count, count * rows, width)


def block_weights(last_all):
    count = last_all.shape[0]
    inclusive = jnp.cumsum(last_all, axis=0)
    exclusive = inclusive - last_all
    inc = jnp.transpose(inclusive, (1, 2, 0))
    exc = jnp.transpose(exclusive, (1, 2, 0))
    row_ids = lax.broadcasted_iota(jnp.int32, (count, count), 0)
    col_ids = lax.broadcasted_iota(jnp.int32, (count, count), 1)
    earlier = col_ids < row_ids
    later = col_ids > row_ids
    forward_gap = exc[..., :, None] - inc[..., None, :]
    backward_gap = exc[..., None, :] - inc[..., :, None]
    forward = jnp.where(earlier, jnp.exp(jnp.where(earlier, forward_gap, 0.0)), 0.0)
    backward = jnp.where(later, jnp.exp(jnp.where(later, backward_gap, 0.0)), 0.0)
    return forward, backward


def mix_blocks(weights, pieces):
    return jnp.einsum(
        "bhcd,dbhrx->cbhrx", weights, pieces, precision=lax.Precision.HIGHEST,
        preferred_element_type=jnp.float32,
    )


def local(query_heads, key_heads, value_heads, grad_out, log_decay):
    batch_count, positions, width_heads = query_heads.shape
    head_count = log_decay.shape[1]
    width = width_heads // head_count
    uly_count = lax.axis_size("uly")
    head_shape = (batch_count, positions, head_count, width)
    q_split = query_heads.reshape(head_shape)
    k_split = key_heads.reshape(head_shape)
    v_split = value_heads.reshape(head_shape)

    rows_in = grad_out.shape[1]
    g_parts = grad_out.reshape(batch_count, rows_in, uly_count, width_heads)
    g_parts = jnp.transpose(g_parts, (2, 0, 1, 3))
    g_parts = lax.all_to_all(g_parts, "uly", 0, 0, tiled=True)
    g_split = jnp.transpose(g_parts, (1, 0, 2, 3)).reshape(head_shape)

    cumulative, last_cum, decay_mask = decay_tables(log_decay)
    rise_rows = to_rows(jnp.exp(cumulative))
    fall_rows = to_rows(jnp.exp(last_cum - cumulative))
    scaled_query = (rise_rows * q_split).astype(jnp.bfloat16)
    scaled_key = (fall_rows * k_split).astype(jnp.bfloat16)
    update = jnp.einsum("bjhd,bjhe->bhde", scaled_key, v_split, preferred_element_type=jnp.float32)

    local_grad = jnp.einsum(
        "bihd,bihe->bhde", scaled_query, g_split, preferred_element_type=jnp.float32
    )
    chip_count = lax.axis_size("z")
    core = lax.axis_index("core")
    second = core == 1
    pairs = [(0, 1), (1, 0)]
    last = last_cum[..., 0]
    own = jnp.where(second, update, local_grad)
    last_row = jnp.broadcast_to(last[..., None, None], (batch_count, head_count, 1, width))
    given = jnp.where(second, local_grad, update)
    other_packed = lax.ppermute(jnp.concatenate([given, last_row], axis=2), "core", pairs)
    other = other_packed[:, :, :width]
    other_last = other_packed[:, :, width, 0]
    keep_mine = jnp.exp(last)[..., None, None]
    keep_other = jnp.exp(other_last)[..., None, None]
    chip_state = keep_mine * other + own
    band = width // chip_count
    chip_last = jnp.broadcast_to((last + other_last)[..., None], (batch_count, head_count, width))
    last_piece = jnp.broadcast_to(
        chip_last[None, :, :, None, :], (chip_count, batch_count, head_count, 1, width)
    )
    send = jnp.concatenate([to_pieces(chip_state, chip_count), last_piece], axis=3)
    got = lax.all_to_all(send, "z", 0, 0, tiled=True)
    forward_w, backward_w = block_weights(got[:, :, :, band, 0])
    weights = jnp.where(second, forward_w, backward_w)
    back = lax.all_to_all(mix_blocks(weights, got[:, :, :, :band]), "z", 0, 0, tiled=True)
    entering = from_pieces(back)
    fixed = (keep_other * entering + other).astype(jnp.bfloat16)
    other_entering = lax.ppermute(entering.astype(jnp.bfloat16), "core", pairs)
    state_b = jnp.where(second, fixed, other_entering)
    carried_b = jnp.where(second, other_entering, fixed)

    scores = jnp.einsum("bihd,bjhd->bhij", q_split, k_split, preferred_element_type=jnp.float32)
    attn_weights = (scores * decay_mask).astype(jnp.bfloat16)
    grad_raw = jnp.einsum("bihe,bjhe->bhij", g_split, v_split, preferred_element_type=jnp.float32)
    grad_scores = (grad_raw * decay_mask).astype(jnp.bfloat16)
    attended = jnp.einsum(
        "bhij,bjhd->bihd", attn_weights, v_split, preferred_element_type=jnp.float32
    )
    attended = attended + jnp.einsum(
        "bihd,bhde->bihe", scaled_query, state_b, preferred_element_type=jnp.float32
    )
    query_part = jnp.einsum(
        "bhij,bjhd->bihd", grad_scores, k_split, preferred_element_type=jnp.float32
    )
    query_part = query_part + rise_rows * jnp.einsum(
        "bihe,bhde->bihd", g_split, state_b, preferred_element_type=jnp.float32
    )
    key_part = jnp.einsum(
        "bhij,bihd->bjhd", grad_scores, q_split, preferred_element_type=jnp.float32
    )
    key_part = key_part + fall_rows * jnp.einsum(
        "bjhe,bhde->bjhd", v_split, carried_b, preferred_element_type=jnp.float32
    )
    value_part = jnp.einsum(
        "bhij,bihe->bjhe", attn_weights, g_split, preferred_element_type=jnp.float32
    )
    value_part = value_part + fall_rows * jnp.einsum(
        "bjhd,bhde->bjhe", k_split, carried_b, preferred_element_type=jnp.float32
    )

    outs = jnp.stack([attended, query_part, key_part, value_part]).astype(jnp.bfloat16)
    outs = outs.reshape(4, batch_count, uly_count, positions // uly_count, width_heads)
    outs = jnp.transpose(outs, (2, 0, 1, 3, 4))
    outs = lax.all_to_all(outs, "uly", 0, 0, tiled=True)

    def to_tokens(index):
        return jnp.transpose(outs[:, index], (1, 2, 0, 3)).reshape(
            batch_count, positions // uly_count, uly_count * width_heads
        )

    return (to_tokens(0), to_tokens(1), to_tokens(2), to_tokens(3))


def solution(mesh):
    ctx_count, uly_count = mesh.shape["ctx"], mesh.shape["uly"]
    grid = mesh.devices.reshape(ctx_count // 2, 2, uly_count)
    chips = Mesh(grid, ("z", "core", "uly"))
    placed = (
        P(None, ("z", "core"), "uly"),
        P(None, ("z", "core"), "uly"),
        P(None, ("z", "core"), "uly"),
        P(None, ("z", "core", "uly"), None),
        P(None, "uly", ("z", "core")),
    )
    return jax.shard_map(
        local,
        mesh=chips,
        in_specs=placed,
        out_specs=(
            P(None, ("z", "core", "uly"), None),
            P(None, ("z", "core", "uly"), None),
            P(None, ("z", "core", "uly"), None),
            P(None, ("z", "core", "uly"), None),
        ),
        check_vma=False,
    )
```

```python
import jax
import jax.numpy as jnp
from jax import lax
from jax.sharding import Mesh, PartitionSpec as P


def decay_tables(log_decay):
    cumulative = jnp.cumsum(log_decay, axis=-1)
    last_cum = cumulative[..., -1:]
    block_len = log_decay.shape[-1]
    row_ids = lax.broadcasted_iota(jnp.int32, (block_len, block_len), 0)
    col_ids = lax.broadcasted_iota(jnp.int32, (block_len, block_len), 1)
    lower_tri = row_ids >= col_ids
    spread = cumulative[..., :, None] - cumulative[..., None, :]
    decay_mask = jnp.where(lower_tri, jnp.exp(jnp.where(lower_tri, spread, 0.0)), 0.0)
    return (cumulative, last_cum, decay_mask)


def to_rows(table):
    return jnp.swapaxes(table, 1, 2)[..., None]


def to_pieces(state, count):
    batch_count, head_count, rows, width = state.shape
    banded = state.reshape(batch_count, head_count, count, rows // count, width)
    return jnp.transpose(banded, (2, 0, 1, 3, 4))


def from_pieces(pieces):
    count, batch_count, head_count, rows, width = pieces.shape
    return jnp.transpose(pieces, (1, 2, 0, 3, 4)).reshape(batch_count, head_count, count * rows, width)


def block_weights(last_all):
    count = last_all.shape[0]
    inclusive = jnp.cumsum(last_all, axis=0)
    exclusive = inclusive - last_all
    inc = jnp.transpose(inclusive, (1, 2, 0))
    exc = jnp.transpose(exclusive, (1, 2, 0))
    row_ids = lax.broadcasted_iota(jnp.int32, (count, count), 0)
    col_ids = lax.broadcasted_iota(jnp.int32, (count, count), 1)
    earlier = col_ids < row_ids
    later = col_ids > row_ids
    forward_gap = exc[..., :, None] - inc[..., None, :]
    backward_gap = exc[..., None, :] - inc[..., :, None]
    forward = jnp.where(earlier, jnp.exp(jnp.where(earlier, forward_gap, 0.0)), 0.0)
    backward = jnp.where(later, jnp.exp(jnp.where(later, backward_gap, 0.0)), 0.0)
    return forward, backward


def mix_blocks(weights, pieces):
    return jnp.einsum(
        "bhcd,dbhrx->cbhrx", weights, pieces, precision=lax.Precision.HIGHEST,
        preferred_element_type=jnp.float32,
    )


def local(query_heads, key_heads, value_heads, grad_out, log_decay):
    batch_count, positions, width_heads = query_heads.shape
    head_count = log_decay.shape[1]
    width = width_heads // head_count
    uly_count = lax.axis_size("uly")
    head_shape = (batch_count, positions, head_count, width)
    q_split = query_heads.reshape(head_shape)
    k_split = key_heads.reshape(head_shape)
    v_split = value_heads.reshape(head_shape)

    rows_in = grad_out.shape[1]
    g_parts = grad_out.reshape(batch_count, rows_in, uly_count, width_heads)
    g_parts = jnp.transpose(g_parts, (2, 0, 1, 3))
    g_parts = lax.all_to_all(g_parts, "uly", 0, 0, tiled=True)
    g_split = jnp.transpose(g_parts, (1, 0, 2, 3)).reshape(head_shape)

    cumulative, last_cum, decay_mask = decay_tables(log_decay)
    rise_rows = to_rows(jnp.exp(cumulative))
    fall_rows = to_rows(jnp.exp(last_cum - cumulative))
    scaled_query = (rise_rows * q_split).astype(jnp.bfloat16)
    scaled_key = (fall_rows * k_split).astype(jnp.bfloat16)
    update = jnp.einsum("bjhd,bjhe->bhde", scaled_key, v_split, preferred_element_type=jnp.float32)

    local_grad = jnp.einsum(
        "bihd,bihe->bhde", scaled_query, g_split, preferred_element_type=jnp.float32
    )
    chip_count = lax.axis_size("z")
    core = lax.axis_index("core")
    second = core == 1
    pairs = [(0, 1), (1, 0)]
    last = last_cum[..., 0]
    own = jnp.where(second, update, local_grad)
    last_row = jnp.broadcast_to(last[..., None, None], (batch_count, head_count, 1, width))
    given = jnp.where(second, local_grad, update)
    other_packed = lax.ppermute(jnp.concatenate([given, last_row], axis=2), "core", pairs)
    other = other_packed[:, :, :width]
    other_last = other_packed[:, :, width, 0]
    keep_mine = jnp.exp(last)[..., None, None]
    keep_other = jnp.exp(other_last)[..., None, None]
    chip_state = keep_mine * other + own
    band = width // chip_count
    chip_last = jnp.broadcast_to((last + other_last)[..., None], (batch_count, head_count, width))
    last_piece = jnp.broadcast_to(
        chip_last[None, :, :, None, :], (chip_count, batch_count, head_count, 1, width)
    )
    send = jnp.concatenate([to_pieces(chip_state, chip_count), last_piece], axis=3)
    got = lax.all_to_all(send, "z", 0, 0, tiled=True)
    forward_w, backward_w = block_weights(got[:, :, :, band, 0])
    weights = jnp.where(second, forward_w, backward_w)
    back = lax.all_to_all(mix_blocks(weights, got[:, :, :, :band]), "z", 0, 0, tiled=True)
    entering = from_pieces(back)
    fixed = (keep_other * entering + other).astype(jnp.bfloat16)
    scores = jnp.einsum("bihd,bjhd->bhij", q_split, k_split, preferred_element_type=jnp.float32)
    attn_weights = (scores * decay_mask).astype(jnp.bfloat16)
    grad_raw = jnp.einsum("bihe,bjhe->bhij", g_split, v_split, preferred_element_type=jnp.float32)
    grad_scores = (grad_raw * decay_mask).astype(jnp.bfloat16)
    attended_inner = jnp.einsum(
        "bhij,bjhd->bihd", attn_weights, v_split, preferred_element_type=jnp.float32
    )
    query_inner = jnp.einsum(
        "bhij,bjhd->bihd", grad_scores, k_split, preferred_element_type=jnp.float32
    )
    key_inner = jnp.einsum(
        "bhij,bihd->bjhd", grad_scores, q_split, preferred_element_type=jnp.float32
    )
    value_inner = jnp.einsum(
        "bhij,bihe->bjhe", attn_weights, g_split, preferred_element_type=jnp.float32
    )

    def forward_pair(state_b):
        attended = attended_inner + jnp.einsum(
            "bihd,bhde->bihe", scaled_query, state_b, preferred_element_type=jnp.float32
        )
        query_part = query_inner + rise_rows * jnp.einsum(
            "bihe,bhde->bihd", g_split, state_b, preferred_element_type=jnp.float32
        )
        return jnp.stack([attended, query_part]).astype(jnp.bfloat16)

    def backward_pair(carried_b):
        key_part = key_inner + fall_rows * jnp.einsum(
            "bjhe,bhde->bjhd", v_split, carried_b, preferred_element_type=jnp.float32
        )
        value_part = value_inner + fall_rows * jnp.einsum(
            "bjhd,bhde->bjhe", k_split, carried_b, preferred_element_type=jnp.float32
        )
        return jnp.stack([key_part, value_part]).astype(jnp.bfloat16)

    def to_tokens(pair):
        outs = pair.reshape(2, batch_count, uly_count, positions // uly_count, width_heads)
        outs = jnp.transpose(outs, (2, 0, 1, 3, 4))
        return lax.all_to_all(outs, "uly", 0, 0, tiled=True)

    ready = to_tokens(jnp.where(second, forward_pair(fixed), backward_pair(fixed)))
    other_entering = lax.ppermute(entering.astype(jnp.bfloat16), "core", pairs)
    later = to_tokens(jnp.where(second, backward_pair(other_entering), forward_pair(other_entering)))
    forward_rows = jnp.where(second, ready, later)
    backward_rows = jnp.where(second, later, ready)

    def rows_of(received, index):
        return jnp.transpose(received[:, index], (1, 2, 0, 3)).reshape(
            batch_count, positions // uly_count, uly_count * width_heads
        )

    return (
        rows_of(forward_rows, 0),
        rows_of(forward_rows, 1),
        rows_of(backward_rows, 0),
        rows_of(backward_rows, 1),
    )


def solution(mesh):
    ctx_count, uly_count = mesh.shape["ctx"], mesh.shape["uly"]
    grid = mesh.devices.reshape(ctx_count // 2, 2, uly_count)
    chips = Mesh(grid, ("z", "core", "uly"))
    placed = (
        P(None, ("z", "core"), "uly"),
        P(None, ("z", "core"), "uly"),
        P(None, ("z", "core"), "uly"),
        P(None, ("z", "core", "uly"), None),
        P(None, "uly", ("z", "core")),
    )
    return jax.shard_map(
        local,
        mesh=chips,
        in_specs=placed,
        out_specs=(
            P(None, ("z", "core", "uly"), None),
            P(None, ("z", "core", "uly"), None),
            P(None, ("z", "core", "uly"), None),
            P(None, ("z", "core", "uly"), None),
        ),
        check_vma=False,
    )
```

```python
import jax
import jax.numpy as jnp
from jax import lax
from jax.sharding import Mesh, PartitionSpec as P


def decay_tables(log_decay):
    cumulative = jnp.cumsum(log_decay, axis=-1)
    last_cum = cumulative[..., -1:]
    block_len = log_decay.shape[-1]
    row_ids = lax.broadcasted_iota(jnp.int32, (block_len, block_len), 0)
    col_ids = lax.broadcasted_iota(jnp.int32, (block_len, block_len), 1)
    lower_tri = row_ids >= col_ids
    spread = cumulative[..., :, None] - cumulative[..., None, :]
    decay_mask = jnp.where(lower_tri, jnp.exp(jnp.where(lower_tri, spread, 0.0)), 0.0)
    return (cumulative, last_cum, decay_mask)


def to_rows(table):
    return jnp.swapaxes(table, 1, 2)[..., None]


def to_pieces(state, count):
    batch_count, head_count, rows, width = state.shape
    banded = state.reshape(batch_count, head_count, count, rows // count, width)
    return jnp.transpose(banded, (2, 0, 1, 3, 4))


def from_pieces(pieces):
    count, batch_count, head_count, rows, width = pieces.shape
    return jnp.transpose(pieces, (1, 2, 0, 3, 4)).reshape(batch_count, head_count, count * rows, width)


def block_weights(last_all):
    count = last_all.shape[0]
    inclusive = jnp.cumsum(last_all, axis=0)
    exclusive = inclusive - last_all
    inc = jnp.transpose(inclusive, (1, 2, 0))
    exc = jnp.transpose(exclusive, (1, 2, 0))
    row_ids = lax.broadcasted_iota(jnp.int32, (count, count), 0)
    col_ids = lax.broadcasted_iota(jnp.int32, (count, count), 1)
    earlier = col_ids < row_ids
    later = col_ids > row_ids
    forward_gap = exc[..., :, None] - inc[..., None, :]
    backward_gap = exc[..., None, :] - inc[..., :, None]
    forward = jnp.where(earlier, jnp.exp(jnp.where(earlier, forward_gap, 0.0)), 0.0)
    backward = jnp.where(later, jnp.exp(jnp.where(later, backward_gap, 0.0)), 0.0)
    return forward, backward


def mix_blocks(weights, pieces):
    return jnp.einsum(
        "bhcd,dbhrx->cbhrx", weights, pieces, precision=lax.Precision.HIGHEST,
        preferred_element_type=jnp.float32,
    )


def local(query_heads, key_heads, value_heads, grad_out, log_decay):
    batch_count, positions, width_heads = query_heads.shape
    head_count = log_decay.shape[1]
    width = width_heads // head_count
    uly_count = lax.axis_size("uly")
    head_shape = (batch_count, positions, head_count, width)
    q_split = query_heads.reshape(head_shape)
    k_split = key_heads.reshape(head_shape)
    v_split = value_heads.reshape(head_shape)

    rows_in = grad_out.shape[1]
    g_parts = grad_out.reshape(batch_count, rows_in, uly_count, width_heads)
    g_parts = jnp.transpose(g_parts, (2, 0, 1, 3))
    g_parts = lax.all_to_all(g_parts, "uly", 0, 0, tiled=True)
    g_split = jnp.transpose(g_parts, (1, 0, 2, 3)).reshape(head_shape)

    cumulative, last_cum, decay_mask = decay_tables(log_decay)
    rise_rows = to_rows(jnp.exp(cumulative))
    fall_rows = to_rows(jnp.exp(last_cum - cumulative))
    scaled_query = (rise_rows * q_split).astype(jnp.bfloat16)
    scaled_key = (fall_rows * k_split).astype(jnp.bfloat16)
    update = jnp.einsum("bjhd,bjhe->bhde", scaled_key, v_split, preferred_element_type=jnp.float32)

    local_grad = jnp.einsum(
        "bihd,bihe->bhde", scaled_query, g_split, preferred_element_type=jnp.float32
    )
    chip_count = lax.axis_size("z")
    core = lax.axis_index("core")
    second = core == 1
    pairs = [(0, 1), (1, 0)]
    last = last_cum[..., 0]
    own = jnp.where(second, update, local_grad)
    last_row = jnp.broadcast_to(last[..., None, None], (batch_count, head_count, 1, width))
    given = jnp.where(second, local_grad, update)
    other_packed = lax.ppermute(jnp.concatenate([given, last_row], axis=2), "core", pairs)
    other = other_packed[:, :, :width]
    other_last = other_packed[:, :, width, 0]
    keep_mine = jnp.exp(last)[..., None, None]
    keep_other = jnp.exp(other_last)[..., None, None]
    chip_state = keep_mine * other + own
    band = width // chip_count
    chip_last = jnp.pad(last + other_last, ((0, 0), (0, width - head_count)))
    last_piece = jnp.broadcast_to(chip_last[None, :, None, :], (chip_count, batch_count, 1, width))
    bands = to_pieces(chip_state, chip_count).reshape(chip_count, batch_count, head_count * band, width)
    got = lax.all_to_all(jnp.concatenate([bands, last_piece], axis=2), "z", 0, 0, tiled=True)
    forward_w, backward_w = block_weights(got[:, :, head_count * band, :head_count])
    weights = jnp.where(second, forward_w, backward_w)
    got_bands = got[:, :, : head_count * band].reshape(chip_count, batch_count, head_count, band, width)
    back = lax.all_to_all(mix_blocks(weights, got_bands), "z", 0, 0, tiled=True)
    entering = from_pieces(back)
    fixed = (keep_other * entering + other).astype(jnp.bfloat16)
    other_entering = lax.ppermute(entering.astype(jnp.bfloat16), "core", pairs)
    state_b = jnp.where(second, fixed, other_entering)
    carried_b = jnp.where(second, other_entering, fixed)

    scores = jnp.einsum("bihd,bjhd->bhij", q_split, k_split, preferred_element_type=jnp.float32)
    attn_weights = (scores * decay_mask).astype(jnp.bfloat16)
    grad_raw = jnp.einsum("bihe,bjhe->bhij", g_split, v_split, preferred_element_type=jnp.float32)
    grad_scores = (grad_raw * decay_mask).astype(jnp.bfloat16)
    attended = jnp.einsum(
        "bhij,bjhd->bihd", attn_weights, v_split, preferred_element_type=jnp.float32
    )
    attended = attended + jnp.einsum(
        "bihd,bhde->bihe", scaled_query, state_b, preferred_element_type=jnp.float32
    )
    query_part = jnp.einsum(
        "bhij,bjhd->bihd", grad_scores, k_split, preferred_element_type=jnp.float32
    )
    query_part = query_part + rise_rows * jnp.einsum(
        "bihe,bhde->bihd", g_split, state_b, preferred_element_type=jnp.float32
    )
    key_part = jnp.einsum(
        "bhij,bihd->bjhd", grad_scores, q_split, preferred_element_type=jnp.float32
    )
    key_part = key_part + fall_rows * jnp.einsum(
        "bjhe,bhde->bjhd", v_split, carried_b, preferred_element_type=jnp.float32
    )
    value_part = jnp.einsum(
        "bhij,bihe->bjhe", attn_weights, g_split, preferred_element_type=jnp.float32
    )
    value_part = value_part + fall_rows * jnp.einsum(
        "bjhd,bhde->bjhe", k_split, carried_b, preferred_element_type=jnp.float32
    )

    outs = jnp.stack([attended, query_part, key_part, value_part]).astype(jnp.bfloat16)
    outs = outs.reshape(4, batch_count, uly_count, positions // uly_count, width_heads)
    outs = jnp.transpose(outs, (2, 0, 1, 3, 4))
    outs = lax.all_to_all(outs, "uly", 0, 0, tiled=True)

    def to_tokens(index):
        return jnp.transpose(outs[:, index], (1, 2, 0, 3)).reshape(
            batch_count, positions // uly_count, uly_count * width_heads
        )

    return (to_tokens(0), to_tokens(1), to_tokens(2), to_tokens(3))


def solution(mesh):
    ctx_count, uly_count = mesh.shape["ctx"], mesh.shape["uly"]
    grid = mesh.devices.reshape(ctx_count // 2, 2, uly_count)
    chips = Mesh(grid, ("z", "core", "uly"))
    placed = (
        P(None, ("z", "core"), "uly"),
        P(None, ("z", "core"), "uly"),
        P(None, ("z", "core"), "uly"),
        P(None, ("z", "core", "uly"), None),
        P(None, "uly", ("z", "core")),
    )
    return jax.shard_map(
        local,
        mesh=chips,
        in_specs=placed,
        out_specs=(
            P(None, ("z", "core", "uly"), None),
            P(None, ("z", "core", "uly"), None),
            P(None, ("z", "core", "uly"), None),
            P(None, ("z", "core", "uly"), None),
        ),
        check_vma=False,
    )
```
